256 devices in a mesh: frame: 16 (over z_lo, y), tensor: 8 (over z_hi, x), dp: 2 (over core).
Axes of the slice: x: 4, y: 4, z: 8 (z_hi: 2, z_lo: 4; z = z_hi * 4 + z_lo), core: 2. Of those that a mesh axis runs over, the one named last changes fastest.
Arguments:
- q_proj: bfloat16 [16384, 3072], P(('dp', 'frame'), 'tensor'), parts along dimension 0
- k_proj: bfloat16 [16384, 3072], P(('dp', 'frame'), 'tensor'), parts along dimension 0
- v_proj: bfloat16 [16384, 3072], P(('dp', 'frame'), 'tensor'), parts along dimension 0, may hold values from -6 to 6
- gain_q: float32 [3072], P('tensor'), may hold values from 0.5 to 6
- gain_k: float32 [3072], P('tensor'), may hold values from 0.5 to 6
- tiles: int32 [128, 12], P('dp'), parts along dimension 0, may hold values from 0 to 63, as said below
Outputs:
- attended: bfloat16 [16384, 3072], P(('dp', 'frame'), 'tensor'), parts along dimension 0
The draws below stay inside these ranges and needn't reach their ends.
There are 2 independent parts, one for each index of `dp`. The reference program is written for one: setup_inputs(seed, part) draws one part's arguments, and reference() takes and returns one part's arrays. A program takes and returns all parts, laid end to end along the dimension named above; an argument that names none is the same for every part. Nothing has to cross between parts.
Inputs may be any that keep to these rules, and one draw needn't show every extreme that they name: `tiles`: row q lists 12 distinct key blocks: q first; then 8 blocks whose slab (group of 4 consecutive blocks, one frame slab) is at most 2 slabs from the slab of q; then 3 blocks that are each the first block of a slab more than 2 slabs away. Farther groups are listed less often.
All inputs are finite; a program needn't handle non-finite values.
Results may differ from the reference program's by a relative error of at most 0.007.
The reference program's roundings to bfloat16 on the way count: a program that leaves them out, or rounds other values in their place, can miss the bound.
Values may be sent and summed in bfloat16 or wider, within the bound.
No kernel may reach another device: no remote copies, remote signals or barrier semaphores. Data moves between devices by JAX's collectives and lax.ppermute only.
A program may use at most 128 MiB of HBM per device.

```python
import math
import jax
import jax.numpy as jnp
from jax import lax

HD = 128
BLK = 128
NEAR = 2
FAR_SLOTS = 3
KSLOTS = 12
TOK_DEV = 512
TOKENS = 8192
NBLK = 64
HEADS = 24


def draw_pair(key):
    width = HEADS * HD
    col_pos = jnp.arange(width, dtype=jnp.float32) / (width - 1)
    rising = 3.0 ** (0.5 * col_pos)
    log_ten = math.log(10.0)

    def scaled(salt):
        noise = jax.random.truncated_normal(jax.random.fold_in(key, salt), -5.0, 5.0, (TOKENS, width), jnp.float32)
        row_scale = jnp.exp(jax.random.uniform(jax.random.fold_in(key, salt + 1), (TOKENS, 1), jnp.float32) * log_ten)
        col_scale = jnp.exp(jax.random.uniform(jax.random.fold_in(key, salt + 2), (1, width), jnp.float32) * log_ten)
        return noise * row_scale * col_scale * rising
    query = scaled(301)
    keyed = scaled(401)
    return (query, keyed)


def draw_q_proj(key, part):
    return draw_pair(key)[0].astype(jnp.bfloat16)


def draw_k_proj(key, part):
    return draw_pair(key)[1].astype(jnp.bfloat16)


def draw_gain(key):
    width = HEADS * HD
    return jnp.exp(jax.random.uniform(key, (width,), jnp.float32, math.log(0.5), math.log(2.0)))


def draw_gain_q(key, part):
    return draw_gain(jax.random.fold_in(key, 11))


def draw_gain_k(key, part):
    return draw_gain(jax.random.fold_in(key, 13))


def draw_tiles(key, part):
    block_count = NBLK
    per_slab = TOK_DEV // BLK
    index = jnp.arange(block_count, dtype=jnp.int32)
    slab = index // per_slab
    distance = jnp.abs(slab[:, None] - slab[None, :])
    near_ok = (distance <= NEAR) & (index[:, None] != index[None, :])
    far_ok = (distance > NEAR) & (index % per_slab == 0)[None, :]
    raw = jax.random.randint(jax.random.fold_in(key, 21), (block_count, block_count), 0, 4096, jnp.int32)
    score = raw // (1 + distance) * block_count + index[None, :]
    near_score = jnp.where(near_ok, score, -1)
    far_score = jnp.where(far_ok, score, -1)
    near_pick = lax.top_k(near_score, KSLOTS - 1 - FAR_SLOTS)[1].astype(jnp.int32)
    far_pick = lax.top_k(far_score, FAR_SLOTS)[1].astype(jnp.int32)
    return jnp.concatenate([index[:, None], near_pick, far_pick], axis=1).astype(jnp.int32)


def levels(key, dims, pieces, smallest, high):
    level = 1.0
    for position, parts in pieces:
        steps = jax.random.uniform(jax.random.fold_in(jax.random.fold_in(key, 6), position), (parts,), jnp.float32, smallest / len(pieces), high / len(pieces))
        level = level * jnp.repeat(jnp.exp(steps), dims[position] // parts).reshape((-1,) + (1,) * (len(dims) - 1 - position))
    return level


def bell_draw(key, shape, scale, reach, cuts=(), kind=jnp.bfloat16):
    array = jax.random.normal(key, shape, jnp.float32) * scale
    if len(cuts) > 0:
        array = levels(key, shape, cuts, -0.22, 0.18) * array
    return jnp.clip(array, min=-reach, max=reach).astype(kind)


def setup_inputs(seed: int = 0, part: int = 0) -> dict:
    streams_of = jax.random.split(jax.random.key(seed), 7)
    own_keys = jax.random.split(jax.random.fold_in(streams_of[6], part), 7)
    return {
        "q_proj": draw_q_proj(jax.random.fold_in(jax.random.fold_in(streams_of[6], part), 71), part),
        "k_proj": draw_k_proj(jax.random.fold_in(jax.random.fold_in(streams_of[6], part), 71), part),
        "v_proj": bell_draw(own_keys[2], (TOKENS, HEADS * HD), 1.0, 6.0, ((0, 16), (1, 8))),
        "gain_q": draw_gain_q(jax.random.fold_in(streams_of[6], 71), part),
        "gain_k": draw_gain_k(jax.random.fold_in(streams_of[6], 71), part),
        "tiles": draw_tiles(jax.random.fold_in(jax.random.fold_in(streams_of[6], part), 71), part),
    }


EPS = 1e-06

def normed(values, gain):
    wide = values.astype(jnp.float32)
    mean_sq = lax.optimization_barrier(jnp.sum(wide * wide, axis=1, keepdims=True)) / wide.shape[1]
    return (wide * lax.rsqrt(mean_sq + EPS) * gain).astype(jnp.bfloat16)

def reference(q_proj, k_proj, v_proj, gain_q, gain_k, tiles):
    width = q_proj.shape[1]
    q_norm = normed(q_proj, gain_q)
    k_norm = normed(k_proj, gain_k)
    q_blocks = q_norm.reshape(NBLK, BLK, HEADS, HD)
    k_blocks = k_norm.reshape(NBLK, BLK, HEADS, HD)
    v_blocks = v_proj.reshape(NBLK, BLK, HEADS, HD)
    scale = 1.0 / math.sqrt(HD)

    def one_block(inputs):
        q_block, listed = inputs
        keys = k_blocks[listed].reshape(KSLOTS * BLK, HEADS, HD)
        values = v_blocks[listed].reshape(KSLOTS * BLK, HEADS, HD)
        scores = jnp.einsum('qhd,khd->hqk', q_block.astype(jnp.float32), keys.astype(jnp.float32)) * scale
        top = lax.optimization_barrier(jnp.max(scores, axis=-1, keepdims=True))
        weights = jnp.exp(scores - top)
        totals = lax.optimization_barrier(jnp.sum(weights, axis=-1))
        rounded = lax.optimization_barrier(weights.astype(jnp.bfloat16))
        summed = jnp.einsum('hqk,khd->hqd', rounded.astype(jnp.float32), values.astype(jnp.float32))
        result = summed / totals[..., None]
        return jnp.transpose(result, (1, 0, 2)).reshape(BLK, width).astype(jnp.bfloat16)
    outputs = lax.map(one_block, (q_blocks, tiles))
    return outputs.reshape(TOKENS, width)
```

```python
import functools
import math

import jax
import jax.numpy as jnp
from jax import lax
from jax.experimental import pallas as pl
from jax.experimental.pallas import tpu as pltpu
from jax.sharding import PartitionSpec as P

HD = 128
BLK = 128
NEAR = 2

EPS = 1e-06


def attn_kernel(idx_ref, q_ref, k_ref, v_ref, o_ref, s_ref, *, heads, slots):
    i = pl.program_id(0)
    scale = 1.0 / math.sqrt(HD)
    for h in range(heads):
        cols = pl.ds(h * HD, HD)
        qh = q_ref[:, cols]
        top = None
        for j in range(slots):
            kb = idx_ref[i, j]
            kh = k_ref[kb, :, cols]
            s = lax.dot_general(
                qh, kh, (((1,), (1,)), ((), ())), preferred_element_type=jnp.float32
            ) * scale
            s_ref[j] = s
            part = jnp.max(s, axis=1, keepdims=True)
            top = part if top is None else jnp.maximum(top, part)
        total = None
        acc = None
        for j in range(slots):
            kb = idx_ref[i, j]
            w = jnp.exp(s_ref[j] - top)
            part = jnp.sum(w, axis=1, keepdims=True)
            total = part if total is None else total + part
            prod = jnp.dot(
                w.astype(jnp.bfloat16), v_ref[kb, :, cols], preferred_element_type=jnp.float32
            )
            acc = prod if acc is None else acc + prod
        o_ref[:, cols] = (acc / total).astype(o_ref.dtype)


def sparse_attend(idx, qn, k_bank, v_bank):
    tok_rows, width = qn.shape
    heads = width // HD
    q_blocks = tok_rows // BLK
    slots = idx.shape[1]
    n_bank = k_bank.shape[0]
    kernel = functools.partial(attn_kernel, heads=heads, slots=slots)
    grid_spec = pltpu.PrefetchScalarGridSpec(
        num_scalar_prefetch=1,
        grid=(q_blocks,),
        in_specs=[
            pl.BlockSpec((BLK, width), lambda i, idx_ref: (i, 0)),
            pl.BlockSpec((n_bank, BLK, width), lambda i, idx_ref: (0, 0, 0)),
            pl.BlockSpec((n_bank, BLK, width), lambda i, idx_ref: (0, 0, 0)),
        ],
        out_specs=pl.BlockSpec((BLK, width), lambda i, idx_ref: (i, 0)),
        scratch_shapes=[pltpu.VMEM((slots, BLK, BLK), jnp.float32)],
    )
    flops = 4 * q_blocks * slots * heads * BLK * BLK * HD
    return pl.pallas_call(
        kernel,
        grid_spec=grid_spec,
        out_shape=jax.ShapeDtypeStruct((tok_rows, width), jnp.bfloat16),
        compiler_params=pltpu.CompilerParams(vmem_limit_bytes=48 * 1024 * 1024),
        cost_estimate=pl.CostEstimate(
            flops=flops,
            transcendentals=q_blocks * slots * heads * BLK * BLK,
            bytes_accessed=2 * (2 * tok_rows * width + 2 * n_bank * BLK * width),
        ),
    )(idx, qn, k_bank, v_bank)


def body(q_proj, k_proj, v_proj, gain_q, gain_k, tiles, *, n_frame):
    tok_rows, width = q_proj.shape
    q_wide = q_proj.astype(jnp.float32)
    k_wide = k_proj.astype(jnp.float32)
    row_sums = lax.psum(
        (jnp.sum(q_wide * q_wide, axis=1), jnp.sum(k_wide * k_wide, axis=1)), "tensor"
    )
    full_width = width * lax.axis_size("tensor")
    q_norm = (q_wide * lax.rsqrt(row_sums[0] / full_width + EPS)[:, None] * gain_q).astype(
        jnp.bfloat16
    )
    k_norm = (k_wide * lax.rsqrt(row_sums[1] / full_width + EPS)[:, None] * gain_k).astype(
        jnp.bfloat16
    )
    blocks = tok_rows // BLK
    frame_pos = lax.axis_index("frame")
    kv_pair = jnp.stack([k_norm, v_proj])

    near = {0: kv_pair}
    for d in range(-NEAR, NEAR + 1):
        if d == 0:
            continue
        perm = [(i, i - d) for i in range(n_frame) if 0 <= i - d < n_frame]
        near[d] = lax.ppermute(kv_pair, "frame", perm)
    far = lax.all_gather(kv_pair[:, :BLK], "frame", axis=0, tiled=False)

    near_k = jnp.concatenate(
        [near[d][0].reshape(blocks, BLK, width) for d in range(-NEAR, NEAR + 1)], axis=0
    )
    near_v = jnp.concatenate(
        [near[d][1].reshape(blocks, BLK, width) for d in range(-NEAR, NEAR + 1)], axis=0
    )
    k_bank = jnp.concatenate([near_k, far[:, 0]], axis=0)
    v_bank = jnp.concatenate([near_v, far[:, 1]], axis=0)
    n_near = (2 * NEAR + 1) * blocks

    q_tiles = lax.dynamic_slice_in_dim(tiles, frame_pos * blocks, blocks, 0)
    key_slab = q_tiles // blocks
    dist = key_slab - frame_pos
    idx = jnp.where(
        jnp.abs(dist) <= NEAR,
        (dist + NEAR) * blocks + q_tiles % blocks,
        n_near + key_slab,
    )
    idx = jnp.clip(idx, 0, n_near + n_frame - 1).astype(jnp.int32)
    return sparse_attend(idx, q_norm, k_bank, v_bank)


def solution(mesh):
    return jax.shard_map(
        functools.partial(body, n_frame=mesh.shape["frame"]),
        mesh=mesh,
        in_specs=(
            P(("dp", "frame"), "tensor"),
            P(("dp", "frame"), "tensor"),
            P(("dp", "frame"), "tensor"),
            P("tensor"),
            P("tensor"),
            P("dp", None),
        ),
        out_specs=P(("dp", "frame"), "tensor"),
        check_vma=False,
    )
```

```python
import functools
import math

import jax
import jax.numpy as jnp
from jax import lax
from jax.experimental import pallas as pl
from jax.experimental.pallas import tpu as pltpu
from jax.sharding import PartitionSpec as P


HD = 128
BLK = 128
NEAR = 2

EPS = 1e-06


def attn_kernel(idx_ref, q_ref, k_ref, v_ref, o_ref, s_ref, *, heads, slots):
    i = pl.program_id(0)
    scale = 1.0 / math.sqrt(HD)
    for h in range(heads):
        cols = pl.ds(h * HD, HD)
        qh = q_ref[:, cols]
        top = None
        for j in range(slots):
            kb = idx_ref[i, j]
            kh = k_ref[kb, :, cols]
            s = lax.dot_general(
                qh, kh, (((1,), (1,)), ((), ())), preferred_element_type=jnp.float32
            ) * scale
            s_ref[j] = s
            part = jnp.max(s, axis=1, keepdims=True)
            top = part if top is None else jnp.maximum(top, part)
        total = None
        acc = None
        for j in range(slots):
            kb = idx_ref[i, j]
            w = jnp.exp(s_ref[j] - top)
            part = jnp.sum(w, axis=1, keepdims=True)
            total = part if total is None else total + part
            prod = jnp.dot(
                w.astype(jnp.bfloat16), v_ref[kb, :, cols], preferred_element_type=jnp.float32
            )
            acc = prod if acc is None else acc + prod
        o_ref[:, cols] = (acc / total).astype(o_ref.dtype)


def sparse_attend(idx, qn, k_bank, v_bank):
    tok_rows, width = qn.shape
    heads = width // HD
    q_blocks = tok_rows // BLK
    slots = idx.shape[1]
    n_bank = k_bank.shape[0]
    kernel = functools.partial(attn_kernel, heads=heads, slots=slots)
    grid_spec = pltpu.PrefetchScalarGridSpec(
        num_scalar_prefetch=1,
        grid=(q_blocks,),
        in_specs=[
            pl.BlockSpec((BLK, width), lambda i, idx_ref: (i, 0)),
            pl.BlockSpec((n_bank, BLK, width), lambda i, idx_ref: (0, 0, 0)),
            pl.BlockSpec((n_bank, BLK, width), lambda i, idx_ref: (0, 0, 0)),
        ],
        out_specs=pl.BlockSpec((BLK, width), lambda i, idx_ref: (i, 0)),
        scratch_shapes=[pltpu.VMEM((slots, BLK, BLK), jnp.float32)],
    )
    flops = 4 * q_blocks * slots * heads * BLK * BLK * HD
    return pl.pallas_call(
        kernel,
        grid_spec=grid_spec,
        out_shape=jax.ShapeDtypeStruct((tok_rows, width), jnp.bfloat16),
        compiler_params=pltpu.CompilerParams(vmem_limit_bytes=48 * 1024 * 1024),
        cost_estimate=pl.CostEstimate(
            flops=flops,
            transcendentals=q_blocks * slots * heads * BLK * BLK,
            bytes_accessed=2 * (2 * tok_rows * width + 2 * n_bank * BLK * width),
        ),
    )(idx, qn, k_bank, v_bank)


def body(q_proj, k_proj, v_proj, gain_q, gain_k, tiles, *, n_frame):
    tok_rows, width = q_proj.shape
    blocks = tok_rows // BLK
    frame_pos = lax.axis_index("frame")
    shifts = [d for d in range(-NEAR, NEAR + 1) if d != 0]

    def exchange(arr):
        tail = arr[BLK:]
        near = {0: tail}
        for d in shifts:
            perm = [(i, i - d) for i in range(n_frame) if 0 <= i - d < n_frame]
            near[d] = lax.ppermute(tail, "frame", perm)
        first = lax.all_gather(arr[:BLK], "frame", axis=0, tiled=False)
        parts = [near[d].reshape(blocks - 1, BLK, width) for d in range(-NEAR, NEAR + 1)]
        return jnp.concatenate(parts + [first], axis=0)

    v_bank = exchange(v_proj)

    q_wide = q_proj.astype(jnp.float32)
    k_wide = k_proj.astype(jnp.float32)
    row_sums = lax.psum(
        (jnp.sum(q_wide * q_wide, axis=1), jnp.sum(k_wide * k_wide, axis=1)), "tensor"
    )
    full_width = width * lax.axis_size("tensor")
    q_norm = (q_wide * lax.rsqrt(row_sums[0] / full_width + EPS)[:, None] * gain_q).astype(
        jnp.bfloat16
    )
    k_norm = (k_wide * lax.rsqrt(row_sums[1] / full_width + EPS)[:, None] * gain_k).astype(
        jnp.bfloat16
    )
    k_bank = exchange(k_norm)
    n_near = (2 * NEAR + 1) * (blocks - 1)

    q_tiles = lax.dynamic_slice_in_dim(tiles, frame_pos * blocks, blocks, 0)
    key_slab = q_tiles // blocks
    within = q_tiles % blocks
    dist = key_slab - frame_pos
    near_ok = (jnp.abs(dist) <= NEAR) & (within > 0)
    idx = jnp.where(
        near_ok,
        (dist + NEAR) * (blocks - 1) + within - 1,
        n_near + key_slab,
    )
    idx = jnp.clip(idx, 0, n_near + n_frame - 1).astype(jnp.int32)
    return sparse_attend(idx, q_norm, k_bank, v_bank)


def solution(mesh):
    return jax.shard_map(
        functools.partial(body, n_frame=mesh.shape["frame"]),
        mesh=mesh,
        in_specs=(
            P(("dp", "frame"), "tensor"),
            P(("dp", "frame"), "tensor"),
            P(("dp", "frame"), "tensor"),
            P("tensor"),
            P("tensor"),
            P("dp", None),
        ),
        out_specs=P(("dp", "frame"), "tensor"),
        check_vma=False,
    )
```

```python
import functools
import math

import jax
import jax.numpy as jnp
from jax import lax
from jax.experimental import pallas as pl
from jax.experimental.pallas import tpu as pltpu
from jax.sharding import PartitionSpec as P


HD = 128
BLK = 128
NEAR = 2

EPS = 1e-06


def attn_kernel(idx_ref, q_ref, k_ref, v_ref, o_ref, s_ref, *, heads, slots):
    i = pl.program_id(0)
    scale = 1.0 / math.sqrt(HD)
    for h in range(heads):
        cols = pl.ds(h * HD, HD)
        qh = q_ref[:, cols]
        top = None
        for j in range(slots):
            kb = idx_ref[i, j]
            kh = k_ref[kb, :, cols]
            s = lax.dot_general(
                qh, kh, (((1,), (1,)), ((), ())), preferred_element_type=jnp.float32
            ) * scale
            s_ref[j] = s
            part = jnp.max(s, axis=1, keepdims=True)
            top = part if top is None else jnp.maximum(top, part)
        total = None
        acc = None
        for j in range(slots):
            kb = idx_ref[i, j]
            w = jnp.exp(s_ref[j] - top)
            part = jnp.sum(w, axis=1, keepdims=True)
            total = part if total is None else total + part
            prod = jnp.dot(
                w.astype(jnp.bfloat16), v_ref[kb, :, cols], preferred_element_type=jnp.float32
            )
            acc = prod if acc is None else acc + prod
        o_ref[:, cols] = (acc / total).astype(o_ref.dtype)


def sparse_attend(idx, qn, k_bank, v_bank):
    tok_rows, width = qn.shape
    heads = width // HD
    q_blocks = tok_rows // BLK
    slots = idx.shape[1]
    n_bank = k_bank.shape[0]
    kernel = functools.partial(attn_kernel, heads=heads, slots=slots)
    grid_spec = pltpu.PrefetchScalarGridSpec(
        num_scalar_prefetch=1,
        grid=(q_blocks,),
        in_specs=[
            pl.BlockSpec((BLK, width), lambda i, idx_ref: (i, 0)),
            pl.BlockSpec((n_bank, BLK, width), lambda i, idx_ref: (0, 0, 0)),
            pl.BlockSpec((n_bank, BLK, width), lambda i, idx_ref: (0, 0, 0)),
        ],
        out_specs=pl.BlockSpec((BLK, width), lambda i, idx_ref: (i, 0)),
        scratch_shapes=[pltpu.VMEM((slots, BLK, BLK), jnp.float32)],
    )
    flops = 4 * q_blocks * slots * heads * BLK * BLK * HD
    return pl.pallas_call(
        kernel,
        grid_spec=grid_spec,
        out_shape=jax.ShapeDtypeStruct((tok_rows, width), jnp.bfloat16),
        compiler_params=pltpu.CompilerParams(vmem_limit_bytes=48 * 1024 * 1024),
        cost_estimate=pl.CostEstimate(
            flops=flops,
            transcendentals=q_blocks * slots * heads * BLK * BLK,
            bytes_accessed=2 * (2 * tok_rows * width + 2 * n_bank * BLK * width),
        ),
    )(idx, qn, k_bank, v_bank)


def body(q_proj, k_proj, v_proj, gain_q, gain_k, tiles, *, n_frame):
    tok_rows, width = q_proj.shape
    blocks = tok_rows // BLK
    frame_pos = lax.axis_index("frame")

    q_wide = q_proj.astype(jnp.float32)
    k_wide = k_proj.astype(jnp.float32)
    row_sums = lax.psum(
        (jnp.sum(q_wide * q_wide, axis=1), jnp.sum(k_wide * k_wide, axis=1)), "tensor"
    )
    full_width = width * lax.axis_size("tensor")
    q_norm = (q_wide * lax.rsqrt(row_sums[0] / full_width + EPS)[:, None] * gain_q).astype(
        jnp.bfloat16
    )
    k_norm = (k_wide * lax.rsqrt(row_sums[1] / full_width + EPS)[:, None] * gain_k).astype(
        jnp.bfloat16
    )
    kv_pair = jnp.stack([k_norm, v_proj])

    offsets = list(range(-NEAR, NEAR + 1))
    near = {0: kv_pair}
    for d in offsets:
        if d != 0:
            perm = [(i, i - d) for i in range(n_frame) if 0 <= i - d < n_frame]
            near[d] = lax.ppermute(kv_pair, "frame", perm)

    held = kv_pair[:, None, :BLK]
    bit = 1
    while bit < n_frame:
        perm = [(i, i ^ bit) for i in range(n_frame)]
        got = lax.ppermute(held, "frame", perm)
        upper = (frame_pos // bit) % 2 == 1
        held = jnp.where(
            upper, jnp.concatenate([got, held], axis=1), jnp.concatenate([held, got], axis=1)
        )
        bit *= 2

    k_bank = jnp.concatenate(
        [near[d][0].reshape(blocks, BLK, width) for d in offsets] + [held[0]], axis=0
    )
    v_bank = jnp.concatenate(
        [near[d][1].reshape(blocks, BLK, width) for d in offsets] + [held[1]], axis=0
    )
    n_near = len(offsets) * blocks

    q_tiles = lax.dynamic_slice_in_dim(tiles, frame_pos * blocks, blocks, 0)
    key_slab = q_tiles // blocks
    dist = key_slab - frame_pos
    idx = jnp.where(
        jnp.abs(dist) <= NEAR,
        (dist + NEAR) * blocks + q_tiles % blocks,
        n_near + key_slab,
    )
    idx = jnp.clip(idx, 0, n_near + n_frame - 1).astype(jnp.int32)
    return sparse_attend(idx, q_norm, k_bank, v_bank)


def solution(mesh):
    return jax.shard_map(
        functools.partial(body, n_frame=mesh.shape["frame"]),
        mesh=mesh,
        in_specs=(
            P(("dp", "frame"), "tensor"),
            P(("dp", "frame"), "tensor"),
            P(("dp", "frame"), "tensor"),
            P("tensor"),
            P("tensor"),
            P("dp", None),
        ),
        out_specs=P(("dp", "frame"), "tensor"),
        check_vma=False,
    )
```

```python
import functools
import math

import jax
import jax.numpy as jnp
from jax import lax
from jax.experimental import pallas as pl
from jax.experimental.pallas import tpu as pltpu
from jax.sharding import PartitionSpec as P


HD = 128
BLK = 128
NEAR = 2

EPS = 1e-06


def attn_kernel(idx_ref, q_ref, k_ref, v_ref, o_ref, s_ref, *, heads, slots):
    i = pl.program_id(0)
    scale = 1.0 / math.sqrt(HD)
    for h in range(heads):
        cols = pl.ds(h * HD, HD)
        qh = q_ref[:, cols]
        top = None
        for j in range(slots):
            kb = idx_ref[i, j]
            kh = k_ref[kb, :, cols]
            s = lax.dot_general(
                qh, kh, (((1,), (1,)), ((), ())), preferred_element_type=jnp.float32
            ) * scale
            s_ref[j] = s
            part = jnp.max(s, axis=1, keepdims=True)
            top = part if top is None else jnp.maximum(top, part)
        total = None
        acc = None
        for j in range(slots):
            kb = idx_ref[i, j]
            w = jnp.exp(s_ref[j] - top)
            part = jnp.sum(w, axis=1, keepdims=True)
            total = part if total is None else total + part
            prod = jnp.dot(
                w.astype(jnp.bfloat16), v_ref[kb, :, cols], preferred_element_type=jnp.float32
            )
            acc = prod if acc is None else acc + prod
        o_ref[:, cols] = (acc / total).astype(o_ref.dtype)


def sparse_attend(idx, qn, k_bank, v_bank):
    tok_rows, width = qn.shape
    heads = width // HD
    q_blocks = tok_rows // BLK
    slots = idx.shape[1]
    n_bank = k_bank.shape[0]
    kernel = functools.partial(attn_kernel, heads=heads, slots=slots)
    grid_spec = pltpu.PrefetchScalarGridSpec(
        num_scalar_prefetch=1,
        grid=(q_blocks,),
        in_specs=[
            pl.BlockSpec((BLK, width), lambda i, idx_ref: (i, 0)),
            pl.BlockSpec((n_bank, BLK, width), lambda i, idx_ref: (0, 0, 0)),
            pl.BlockSpec((n_bank, BLK, width), lambda i, idx_ref: (0, 0, 0)),
        ],
        out_specs=pl.BlockSpec((BLK, width), lambda i, idx_ref: (i, 0)),
        scratch_shapes=[pltpu.VMEM((slots, BLK, BLK), jnp.float32)],
    )
    flops = 4 * q_blocks * slots * heads * BLK * BLK * HD
    return pl.pallas_call(
        kernel,
        grid_spec=grid_spec,
        out_shape=jax.ShapeDtypeStruct((tok_rows, width), jnp.bfloat16),
        compiler_params=pltpu.CompilerParams(vmem_limit_bytes=48 * 1024 * 1024),
        cost_estimate=pl.CostEstimate(
            flops=flops,
            transcendentals=q_blocks * slots * heads * BLK * BLK,
            bytes_accessed=2 * (2 * tok_rows * width + 2 * n_bank * BLK * width),
        ),
    )(idx, qn, k_bank, v_bank)


def xor_gather(piece, n_frame, frame_pos):
    held = piece[None]
    bit = 1
    while bit < n_frame:
        perm = [(i, i ^ bit) for i in range(n_frame)]
        got = lax.ppermute(held, "frame", perm)
        upper = (frame_pos // bit) % 2 == 1
        held = jnp.where(
            upper, jnp.concatenate([got, held], axis=0), jnp.concatenate([held, got], axis=0)
        )
        bit *= 2
    return held


def body(q_proj, k_proj, v_proj, gain_q, gain_k, tiles, *, n_frame):
    tok_rows, width = q_proj.shape
    blocks = tok_rows // BLK
    frame_pos = lax.axis_index("frame")
    full_width = width * lax.axis_size("tensor")
    offsets = list(range(-NEAR, NEAR + 1))
    perms = {
        d: [(i, i - d) for i in range(n_frame) if 0 <= i - d < n_frame] for d in offsets if d != 0
    }

    kv_raw = jnp.stack([k_proj, v_proj])
    first = lax.all_gather(kv_raw[:, :BLK], "frame", axis=1, tiled=False)
    tail = kv_raw[:, BLK:]
    near = {0: tail}
    for d in perms:
        near[d] = lax.ppermute(tail, "frame", perms[d])

    q_wide = q_proj.astype(jnp.float32)
    k_wide = k_proj.astype(jnp.float32)
    row_sums = lax.psum(
        (jnp.sum(q_wide * q_wide, axis=1), jnp.sum(k_wide * k_wide, axis=1)), "tensor"
    )
    q_norm = (q_wide * lax.rsqrt(row_sums[0] / full_width + EPS)[:, None] * gain_q).astype(
        jnp.bfloat16
    )
    k_sum = row_sums[1]
    sum_tail = k_sum[BLK:]
    near_sum = {0: sum_tail}
    for d in perms:
        near_sum[d] = lax.ppermute(sum_tail, "frame", perms[d])
    first_sum = xor_gather(k_sum[:BLK], n_frame, frame_pos)

    bank_sum = jnp.concatenate(
        [near_sum[d].reshape(blocks - 1, BLK) for d in offsets] + [first_sum], axis=0
    )
    k_scale = lax.rsqrt(bank_sum / full_width + EPS)[:, :, None]
    k_raw = jnp.concatenate(
        [near[d][0].reshape(blocks - 1, BLK, width) for d in offsets] + [first[0]], axis=0
    )
    k_bank = (k_raw.astype(jnp.float32) * k_scale * gain_k).astype(jnp.bfloat16)
    v_bank = jnp.concatenate(
        [near[d][1].reshape(blocks - 1, BLK, width) for d in offsets] + [first[1]], axis=0
    )
    n_near = len(offsets) * (blocks - 1)

    q_tiles = lax.dynamic_slice_in_dim(tiles, frame_pos * blocks, blocks, 0)
    key_slab = q_tiles // blocks
    within = q_tiles % blocks
    dist = key_slab - frame_pos
    near_ok = (jnp.abs(dist) <= NEAR) & (within > 0)
    idx = jnp.where(
        near_ok,
        (dist + NEAR) * (blocks - 1) + within - 1,
        n_near + key_slab,
    )
    idx = jnp.clip(idx, 0, n_near + n_frame - 1).astype(jnp.int32)
    return sparse_attend(idx, q_norm, k_bank, v_bank)


def solution(mesh):
    return jax.shard_map(
        functools.partial(body, n_frame=mesh.shape["frame"]),
        mesh=mesh,
        in_specs=(
            P(("dp", "frame"), "tensor"),
            P(("dp", "frame"), "tensor"),
            P(("dp", "frame"), "tensor"),
            P("tensor"),
            P("tensor"),
            P("dp", None),
        ),
        out_specs=P(("dp", "frame"), "tensor"),
        check_vma=False,
    )
```

```python
import functools
import math

import jax
import jax.numpy as jnp
from jax import lax
from jax.experimental import pallas as pl
from jax.experimental.pallas import tpu as pltpu
from jax.sharding import PartitionSpec as P


HD = 128
BLK = 128
NEAR = 2

EPS = 1e-06


def attn_kernel(idx_ref, q_ref, k_ref, v_ref, o_ref, s_ref, *, heads, slots):
    i = pl.program_id(0)
    scale = 1.0 / math.sqrt(HD)
    for h in range(heads):
        cols = pl.ds(h * HD, HD)
        qh = q_ref[:, cols]
        top = None
        for j in range(slots):
            kb = idx_ref[i, j]
            kh = k_ref[kb, :, cols]
            s = lax.dot_general(
                qh, kh, (((1,), (1,)), ((), ())), preferred_element_type=jnp.float32
            ) * scale
            s_ref[j] = s
            part = jnp.max(s, axis=1, keepdims=True)
            top = part if top is None else jnp.maximum(top, part)
        total = None
        acc = None
        for j in range(slots):
            kb = idx_ref[i, j]
            w = jnp.exp(s_ref[j] - top)
            part = jnp.sum(w, axis=1, keepdims=True)
            total = part if total is None else total + part
            prod = jnp.dot(
                w.astype(jnp.bfloat16), v_ref[kb, :, cols], preferred_element_type=jnp.float32
            )
            acc = prod if acc is None else acc + prod
        o_ref[:, cols] = (acc / total).astype(o_ref.dtype)


def sparse_attend(idx, qn, k_bank, v_bank):
    tok_rows, width = qn.shape
    heads = width // HD
    q_blocks = tok_rows // BLK
    slots = idx.shape[1]
    n_bank = k_bank.shape[0]
    kernel = functools.partial(attn_kernel, heads=heads, slots=slots)
    grid_spec = pltpu.PrefetchScalarGridSpec(
        num_scalar_prefetch=1,
        grid=(q_blocks,),
        in_specs=[
            pl.BlockSpec((BLK, width), lambda i, idx_ref: (i, 0)),
            pl.BlockSpec((n_bank, BLK, width), lambda i, idx_ref: (0, 0, 0)),
            pl.BlockSpec((n_bank, BLK, width), lambda i, idx_ref: (0, 0, 0)),
        ],
        out_specs=pl.BlockSpec((BLK, width), lambda i, idx_ref: (i, 0)),
        scratch_shapes=[pltpu.VMEM((slots, BLK, BLK), jnp.float32)],
    )
    flops = 4 * q_blocks * slots * heads * BLK * BLK * HD
    return pl.pallas_call(
        kernel,
        grid_spec=grid_spec,
        out_shape=jax.ShapeDtypeStruct((tok_rows, width), jnp.bfloat16),
        compiler_params=pltpu.CompilerParams(vmem_limit_bytes=48 * 1024 * 1024),
        cost_estimate=pl.CostEstimate(
            flops=flops,
            transcendentals=q_blocks * slots * heads * BLK * BLK,
            bytes_accessed=2 * (2 * tok_rows * width + 2 * n_bank * BLK * width),
        ),
    )(idx, qn, k_bank, v_bank)


def xor_gather(piece, n_frame, frame_pos):
    held = piece[None]
    bit = 1
    while bit < n_frame:
        perm = [(i, i ^ bit) for i in range(n_frame)]
        got = lax.ppermute(held, "frame", perm)
        upper = (frame_pos // bit) % 2 == 1
        held = jnp.where(
            upper, jnp.concatenate([got, held], axis=0), jnp.concatenate([held, got], axis=0)
        )
        bit *= 2
    return held


def body(q_proj, k_proj, v_proj, gain_q, gain_k, tiles, *, n_frame):
    tok_rows, width = q_proj.shape
    blocks = tok_rows // BLK
    frame_pos = lax.axis_index("frame")
    full_width = width * lax.axis_size("tensor")
    offsets = list(range(-NEAR, NEAR + 1))
    perms = {
        d: [(i, i - d) for i in range(n_frame) if 0 <= i - d < n_frame] for d in offsets if d != 0
    }

    kv_raw = jnp.stack([k_proj, v_proj])
    first = lax.all_gather(kv_raw[:, :BLK], "frame", axis=1, tiled=False)
    tail = kv_raw[:, BLK:]
    near = {0: tail}
    for d in perms:
        near[d] = lax.ppermute(tail, "frame", perms[d])

    q_wide = q_proj.astype(jnp.float32)
    k_wide = k_proj.astype(jnp.float32)
    row_sums = lax.psum(
        (jnp.sum(q_wide * q_wide, axis=1), jnp.sum(k_wide * k_wide, axis=1)), "tensor"
    )
    q_norm = (q_wide * lax.rsqrt(row_sums[0] / full_width + EPS)[:, None] * gain_q).astype(
        jnp.bfloat16
    )
    k_sum = row_sums[1]
    all_sum = xor_gather(k_sum, n_frame, frame_pos)
    near_slab = jnp.clip(frame_pos + jnp.array(offsets), 0, n_frame - 1)
    near_sum = all_sum[near_slab][:, BLK:].reshape(len(offsets) * (blocks - 1), BLK)
    bank_sum = jnp.concatenate([near_sum, all_sum[:, :BLK]], axis=0)
    k_scale = lax.rsqrt(bank_sum / full_width + EPS)[:, :, None]
    k_raw = jnp.concatenate(
        [near[d][0].reshape(blocks - 1, BLK, width) for d in offsets] + [first[0]], axis=0
    )
    k_bank = (k_raw.astype(jnp.float32) * k_scale * gain_k).astype(jnp.bfloat16)
    v_bank = jnp.concatenate(
        [near[d][1].reshape(blocks - 1, BLK, width) for d in offsets] + [first[1]], axis=0
    )
    n_near = len(offsets) * (blocks - 1)

    q_tiles = lax.dynamic_slice_in_dim(tiles, frame_pos * blocks, blocks, 0)
    key_slab = q_tiles // blocks
    within = q_tiles % blocks
    dist = key_slab - frame_pos
    near_ok = (jnp.abs(dist) <= NEAR) & (within > 0)
    idx = jnp.where(
        near_ok,
        (dist + NEAR) * (blocks - 1) + within - 1,
        n_near + key_slab,
    )
    idx = jnp.clip(idx, 0, n_near + n_frame - 1).astype(jnp.int32)
    return sparse_attend(idx, q_norm, k_bank, v_bank)


def solution(mesh):
    return jax.shard_map(
        functools.partial(body, n_frame=mesh.shape["frame"]),
        mesh=mesh,
        in_specs=(
            P(("dp", "frame"), "tensor"),
            P(("dp", "frame"), "tensor"),
            P(("dp", "frame"), "tensor"),
            P("tensor"),
            P("tensor"),
            P("dp", None),
        ),
        out_specs=P(("dp", "frame"), "tensor"),
        check_vma=False,
    )
```

```python
import functools
import math

import jax
import jax.numpy as jnp
from jax import lax
from jax.experimental import pallas as pl
from jax.experimental.pallas import tpu as pltpu
from jax.sharding import PartitionSpec as P


HD = 128
BLK = 128
NEAR = 2

EPS = 1e-06


def attn_kernel(sel_ref, q_ref, kn_ref, vn_ref, kf_ref, vf_ref, o_ref, s_ref, *, q_blocks, slots):
    scale = 1.0 / math.sqrt(HD)
    for b in range(q_blocks):
        qh = q_ref[pl.ds(b * BLK, BLK), :]
        top = None
        for j in range(slots):
            use_near = sel_ref[0, b, j] == 1
            kh = jnp.where(use_near, kn_ref[sel_ref[1, b, j]], kf_ref[sel_ref[2, b, j]])
            s = lax.dot_general(
                qh, kh, (((1,), (1,)), ((), ())), preferred_element_type=jnp.float32
            ) * scale
            s_ref[j] = s
            top = s if top is None else jnp.maximum(top, s)
        top = jnp.max(top, axis=1, keepdims=True)
        total = None
        acc = None
        for j in range(slots):
            use_near = sel_ref[0, b, j] == 1
            vh = jnp.where(use_near, vn_ref[sel_ref[1, b, j]], vf_ref[0, sel_ref[2, b, j]])
            w = jnp.exp(s_ref[j] - top)
            total = w if total is None else total + w
            prod = jnp.dot(w.astype(jnp.bfloat16), vh, preferred_element_type=jnp.float32)
            acc = prod if acc is None else acc + prod
        total = jnp.sum(total, axis=1, keepdims=True)
        o_ref[pl.ds(b * BLK, BLK), :] = (acc / total).astype(o_ref.dtype)


def sparse_attend(sel, qn, kn_near, v_near, kn_first, first):
    tok_rows, width = qn.shape
    heads = width // HD
    q_blocks = tok_rows // BLK
    slots = sel.shape[2]
    n_near = kn_near.shape[0]
    n_first = kn_first.shape[0]
    kernel = functools.partial(attn_kernel, q_blocks=q_blocks, slots=slots)
    grid_spec = pltpu.PrefetchScalarGridSpec(
        num_scalar_prefetch=1,
        grid=(heads,),
        in_specs=[
            pl.BlockSpec((tok_rows, HD), lambda h, sel_ref: (0, h)),
            pl.BlockSpec((n_near, BLK, HD), lambda h, sel_ref: (0, 0, h)),
            pl.BlockSpec((n_near, BLK, HD), lambda h, sel_ref: (0, 0, h)),
            pl.BlockSpec((n_first, BLK, HD), lambda h, sel_ref: (0, 0, h)),
            pl.BlockSpec((1, n_first, BLK, HD), lambda h, sel_ref: (1, 0, 0, h)),
        ],
        out_specs=pl.BlockSpec((tok_rows, HD), lambda h, sel_ref: (0, h)),
        scratch_shapes=[pltpu.VMEM((slots, BLK, BLK), jnp.float32)],
    )
    flops = 4 * q_blocks * slots * heads * BLK * BLK * HD
    return pl.pallas_call(
        kernel,
        grid_spec=grid_spec,
        out_shape=jax.ShapeDtypeStruct((tok_rows, width), jnp.bfloat16),
        compiler_params=pltpu.CompilerParams(vmem_limit_bytes=48 * 1024 * 1024),
        cost_estimate=pl.CostEstimate(
            flops=flops,
            transcendentals=q_blocks * slots * heads * BLK * BLK,
            bytes_accessed=2 * (2 * tok_rows * width + 2 * (n_near + n_first) * BLK * width),
        ),
    )(sel, qn, kn_near, v_near, kn_first, first)


def xor_gather(piece, n_frame, frame_pos):
    held = piece[None]
    bit = 1
    while bit < n_frame:
        perm = [(i, i ^ bit) for i in range(n_frame)]
        got = lax.ppermute(held, "frame", perm)
        upper = (frame_pos // bit) % 2 == 1
        held = jnp.where(
            upper, jnp.concatenate([got, held], axis=0), jnp.concatenate([held, got], axis=0)
        )
        bit *= 2
    return held


def body(q_proj, k_proj, v_proj, gain_q, gain_k, tiles, *, n_frame):
    tok_rows, width = q_proj.shape
    blocks = tok_rows // BLK
    frame_pos = lax.axis_index("frame")
    full_width = width * lax.axis_size("tensor")
    offsets = list(range(-NEAR, NEAR + 1))
    perms = {
        d: [(i, i - d) for i in range(n_frame) if 0 <= i - d < n_frame] for d in offsets if d != 0
    }

    kv_raw = jnp.stack([k_proj, v_proj])
    first = lax.all_gather(kv_raw[:, :BLK], "frame", axis=1, tiled=False)
    tail = kv_raw[:, BLK:]
    near = {0: tail}
    for d in perms:
        near[d] = lax.ppermute(tail, "frame", perms[d])

    q_wide = q_proj.astype(jnp.float32)
    k_wide = k_proj.astype(jnp.float32)
    row_sums = lax.psum(
        (jnp.sum(q_wide * q_wide, axis=1), jnp.sum(k_wide * k_wide, axis=1)), "tensor"
    )
    q_norm = (q_wide * lax.rsqrt(row_sums[0] / full_width + EPS)[:, None] * gain_q).astype(
        jnp.bfloat16
    )
    k_sum = row_sums[1]
    all_sum = xor_gather(k_sum, n_frame, frame_pos)
    near_slab = jnp.clip(frame_pos + jnp.array(offsets), 0, n_frame - 1)
    near_sum = all_sum[near_slab][:, BLK:].reshape(len(offsets) * (blocks - 1), BLK)
    near_scale = lax.rsqrt(near_sum / full_width + EPS)[:, :, None]
    first_scale = lax.rsqrt(all_sum[:, :BLK] / full_width + EPS)[:, :, None]
    k_near = jnp.concatenate(
        [near[d][0].reshape(blocks - 1, BLK, width) for d in offsets], axis=0
    )
    kn_near = (k_near.astype(jnp.float32) * near_scale * gain_k).astype(jnp.bfloat16)
    v_near = jnp.concatenate(
        [near[d][1].reshape(blocks - 1, BLK, width) for d in offsets], axis=0
    )
    kn_first = (first[0].astype(jnp.float32) * first_scale * gain_k).astype(jnp.bfloat16)

    q_tiles = lax.dynamic_slice_in_dim(tiles, frame_pos * blocks, blocks, 0)
    key_slab = q_tiles // blocks
    within = q_tiles % blocks
    dist = key_slab - frame_pos
    near_ok = (jnp.abs(dist) <= NEAR) & (within > 0)
    near_idx = jnp.clip((dist + NEAR) * (blocks - 1) + within - 1, 0, len(offsets) * (blocks - 1) - 1)
    first_idx = jnp.clip(key_slab, 0, n_frame - 1)
    sel = jnp.stack([near_ok.astype(jnp.int32), near_idx, first_idx]).astype(jnp.int32)
    return sparse_attend(sel, q_norm, kn_near, v_near, kn_first, first)


def solution(mesh):
    return jax.shard_map(
        functools.partial(body, n_frame=mesh.shape["frame"]),
        mesh=mesh,
        in_specs=(
            P(("dp", "frame"), "tensor"),
            P(("dp", "frame"), "tensor"),
            P(("dp", "frame"), "tensor"),
            P("tensor"),
            P("tensor"),
            P("dp", None),
        ),
        out_specs=P(("dp", "frame"), "tensor"),
        check_vma=False,
    )
```

```python
import functools
import math

import jax
import jax.numpy as jnp
from jax import lax
from jax.experimental import pallas as pl
from jax.experimental.pallas import tpu as pltpu
from jax.sharding import PartitionSpec as P


HD = 128
BLK = 128
NEAR = 2

EPS = 1e-06


def attn_kernel(sel_ref, q_ref, kn_ref, vn_ref, kf_ref, vf_ref, o_ref, kc_ref, vc_ref, *, q_blocks, slots):
    scale = 1.0 / math.sqrt(HD)
    for b in range(q_blocks):
        for j in range(slots):
            use_near = sel_ref[0, b, j] == 1
            rows = pl.ds(j * BLK, BLK)
            kc_ref[rows, :] = jnp.where(use_near, kn_ref[sel_ref[1, b, j]], kf_ref[sel_ref[2, b, j]])
            vc_ref[rows, :] = jnp.where(
                use_near, vn_ref[sel_ref[1, b, j]], vf_ref[0, sel_ref[2, b, j]]
            )
        qh = q_ref[pl.ds(b * BLK, BLK), :]
        s = lax.dot_general(
            qh, kc_ref[...], (((1,), (1,)), ((), ())), preferred_element_type=jnp.float32
        ) * scale
        top = jnp.max(s, axis=1, keepdims=True)
        w = jnp.exp(s - top)
        total = jnp.sum(w, axis=1, keepdims=True)
        acc = jnp.dot(w.astype(jnp.bfloat16), vc_ref[...], preferred_element_type=jnp.float32)
        o_ref[pl.ds(b * BLK, BLK), :] = (acc / total).astype(o_ref.dtype)


def sparse_attend(sel, qn, kn_near, v_near, kn_first, first):
    tok_rows, width = qn.shape
    heads = width // HD
    q_blocks = tok_rows // BLK
    slots = sel.shape[2]
    n_near = kn_near.shape[0]
    n_first = kn_first.shape[0]
    kernel = functools.partial(attn_kernel, q_blocks=q_blocks, slots=slots)
    grid_spec = pltpu.PrefetchScalarGridSpec(
        num_scalar_prefetch=1,
        grid=(heads,),
        in_specs=[
            pl.BlockSpec((tok_rows, HD), lambda h, sel_ref: (0, h)),
            pl.BlockSpec((n_near, BLK, HD), lambda h, sel_ref: (0, 0, h)),
            pl.BlockSpec((n_near, BLK, HD), lambda h, sel_ref: (0, 0, h)),
            pl.BlockSpec((n_first, BLK, HD), lambda h, sel_ref: (0, 0, h)),
            pl.BlockSpec((1, n_first, BLK, HD), lambda h, sel_ref: (1, 0, 0, h)),
        ],
        out_specs=pl.BlockSpec((tok_rows, HD), lambda h, sel_ref: (0, h)),
        scratch_shapes=[
            pltpu.VMEM((slots * BLK, HD), jnp.bfloat16),
            pltpu.VMEM((slots * BLK, HD), jnp.bfloat16),
        ],
    )
    flops = 4 * q_blocks * slots * heads * BLK * BLK * HD
    return pl.pallas_call(
        kernel,
        grid_spec=grid_spec,
        out_shape=jax.ShapeDtypeStruct((tok_rows, width), jnp.bfloat16),
        compiler_params=pltpu.CompilerParams(vmem_limit_bytes=48 * 1024 * 1024),
        cost_estimate=pl.CostEstimate(
            flops=flops,
            transcendentals=q_blocks * slots * heads * BLK * BLK,
            bytes_accessed=2 * (2 * tok_rows * width + 2 * (n_near + n_first) * BLK * width),
        ),
    )(sel, qn, kn_near, v_near, kn_first, first)


def xor_gather(piece, n_frame, frame_pos):
    held = piece[None]
    bit = 1
    while bit < n_frame:
        perm = [(i, i ^ bit) for i in range(n_frame)]
        got = lax.ppermute(held, "frame", perm)
        upper = (frame_pos // bit) % 2 == 1
        held = jnp.where(
            upper, jnp.concatenate([got, held], axis=0), jnp.concatenate([held, got], axis=0)
        )
        bit *= 2
    return held


def body(q_proj, k_proj, v_proj, gain_q, gain_k, tiles, *, n_frame):
    tok_rows, width = q_proj.shape
    blocks = tok_rows // BLK
    frame_pos = lax.axis_index("frame")
    full_width = width * lax.axis_size("tensor")
    offsets = list(range(-NEAR, NEAR + 1))
    perms = {
        d: [(i, i - d) for i in range(n_frame) if 0 <= i - d < n_frame] for d in offsets if d != 0
    }

    kv_raw = jnp.stack([k_proj, v_proj])
    first = lax.all_gather(kv_raw[:, :BLK], "frame", axis=1, tiled=False)
    tail = kv_raw[:, BLK:]
    near = {0: tail}
    for d in perms:
        near[d] = lax.ppermute(tail, "frame", perms[d])

    q_wide = q_proj.astype(jnp.float32)
    k_wide = k_proj.astype(jnp.float32)
    row_sums = lax.psum(
        (jnp.sum(q_wide * q_wide, axis=1), jnp.sum(k_wide * k_wide, axis=1)), "tensor"
    )
    q_norm = (q_wide * lax.rsqrt(row_sums[0] / full_width + EPS)[:, None] * gain_q).astype(
        jnp.bfloat16
    )
    k_sum = row_sums[1]
    all_sum = xor_gather(k_sum, n_frame, frame_pos)
    near_slab = jnp.clip(frame_pos + jnp.array(offsets), 0, n_frame - 1)
    near_sum = all_sum[near_slab][:, BLK:].reshape(len(offsets) * (blocks - 1), BLK)
    near_scale = lax.rsqrt(near_sum / full_width + EPS)[:, :, None]
    first_scale = lax.rsqrt(all_sum[:, :BLK] / full_width + EPS)[:, :, None]
    k_near = jnp.concatenate(
        [near[d][0].reshape(blocks - 1, BLK, width) for d in offsets], axis=0
    )
    kn_near = (k_near.astype(jnp.float32) * near_scale * gain_k).astype(jnp.bfloat16)
    v_near = jnp.concatenate(
        [near[d][1].reshape(blocks - 1, BLK, width) for d in offsets], axis=0
    )
    kn_first = (first[0].astype(jnp.float32) * first_scale * gain_k).astype(jnp.bfloat16)

    q_tiles = lax.dynamic_slice_in_dim(tiles, frame_pos * blocks, blocks, 0)
    key_slab = q_tiles // blocks
    within = q_tiles % blocks
    dist = key_slab - frame_pos
    near_ok = (jnp.abs(dist) <= NEAR) & (within > 0)
    near_idx = jnp.clip((dist + NEAR) * (blocks - 1) + within - 1, 0, len(offsets) * (blocks - 1) - 1)
    first_idx = jnp.clip(key_slab, 0, n_frame - 1)
    sel = jnp.stack([near_ok.astype(jnp.int32), near_idx, first_idx]).astype(jnp.int32)
    return sparse_attend(sel, q_norm, kn_near, v_near, kn_first, first)


def solution(mesh):
    return jax.shard_map(
        functools.partial(body, n_frame=mesh.shape["frame"]),
        mesh=mesh,
        in_specs=(
            P(("dp", "frame"), "tensor"),
            P(("dp", "frame"), "tensor"),
            P(("dp", "frame"), "tensor"),
            P("tensor"),
            P("tensor"),
            P("dp", None),
        ),
        out_specs=P(("dp", "frame"), "tensor"),
        check_vma=False,
    )
```

```python
import functools
import math

import jax
import jax.numpy as jnp
from jax import lax
from jax.experimental import pallas as pl
from jax.experimental.pallas import tpu as pltpu
from jax.sharding import PartitionSpec as P


HD = 128
BLK = 128
NEAR = 2

EPS = 1e-06


def attn_kernel(sel_ref, q_ref, kn_ref, vn_ref, kf_ref, vf_ref, o_ref, kc_ref, vc_ref, *, q_blocks, slots):
    scale = 1.0 / math.sqrt(HD)
    for b in range(q_blocks):
        for j in range(slots):
            use_near = sel_ref[0, b, j] == 1
            rows = pl.ds(j * BLK, BLK)
            kc_ref[rows, :] = jnp.where(use_near, kn_ref[sel_ref[1, b, j]], kf_ref[sel_ref[2, b, j]])
            vc_ref[rows, :] = jnp.where(
                use_near, vn_ref[sel_ref[1, b, j]], vf_ref[0, sel_ref[2, b, j]]
            )
        qh = q_ref[pl.ds(b * BLK, BLK), :]
        s = lax.dot_general(
            kc_ref[...], qh, (((1,), (1,)), ((), ())), preferred_element_type=jnp.float32
        ) * scale
        top = jnp.max(s, axis=0, keepdims=True)
        w = jnp.exp(s - top)
        total = jnp.sum(w, axis=0, keepdims=True)
        acc = lax.dot_general(
            w.astype(jnp.bfloat16), vc_ref[...], (((0,), (0,)), ((), ())),
            preferred_element_type=jnp.float32,
        )
        total = jnp.transpose(jnp.broadcast_to(total, (BLK, BLK)))
        o_ref[pl.ds(b * BLK, BLK), :] = (acc / total).astype(o_ref.dtype)


def sparse_attend(sel, qn, kn_near, v_near, kn_first, first):
    tok_rows, width = qn.shape
    heads = width // HD
    q_blocks = tok_rows // BLK
    slots = sel.shape[2]
    n_near = kn_near.shape[0]
    n_first = kn_first.shape[0]
    kernel = functools.partial(attn_kernel, q_blocks=q_blocks, slots=slots)
    grid_spec = pltpu.PrefetchScalarGridSpec(
        num_scalar_prefetch=1,
        grid=(heads,),
        in_specs=[
            pl.BlockSpec((tok_rows, HD), lambda h, sel_ref: (0, h)),
            pl.BlockSpec((n_near, BLK, HD), lambda h, sel_ref: (0, 0, h)),
            pl.BlockSpec((n_near, BLK, HD), lambda h, sel_ref: (0, 0, h)),
            pl.BlockSpec((n_first, BLK, HD), lambda h, sel_ref: (0, 0, h)),
            pl.BlockSpec((1, n_first, BLK, HD), lambda h, sel_ref: (1, 0, 0, h)),
        ],
        out_specs=pl.BlockSpec((tok_rows, HD), lambda h, sel_ref: (0, h)),
        scratch_shapes=[
            pltpu.VMEM((slots * BLK, HD), jnp.bfloat16),
            pltpu.VMEM((slots * BLK, HD), jnp.bfloat16),
        ],
    )
    flops = 4 * q_blocks * slots * heads * BLK * BLK * HD
    return pl.pallas_call(
        kernel,
        grid_spec=grid_spec,
        out_shape=jax.ShapeDtypeStruct((tok_rows, width), jnp.bfloat16),
        compiler_params=pltpu.CompilerParams(vmem_limit_bytes=48 * 1024 * 1024),
        cost_estimate=pl.CostEstimate(
            flops=flops,
            transcendentals=q_blocks * slots * heads * BLK * BLK,
            bytes_accessed=2 * (2 * tok_rows * width + 2 * (n_near + n_first) * BLK * width),
        ),
    )(sel, qn, kn_near, v_near, kn_first, first)


def xor_gather(piece, n_frame, frame_pos):
    held = piece[None]
    bit = 1
    while bit < n_frame:
        perm = [(i, i ^ bit) for i in range(n_frame)]
        got = lax.ppermute(held, "frame", perm)
        upper = (frame_pos // bit) % 2 == 1
        held = jnp.where(
            upper, jnp.concatenate([got, held], axis=0), jnp.concatenate([held, got], axis=0)
        )
        bit *= 2
    return held


def body(q_proj, k_proj, v_proj, gain_q, gain_k, tiles, *, n_frame):
    tok_rows, width = q_proj.shape
    blocks = tok_rows // BLK
    frame_pos = lax.axis_index("frame")
    full_width = width * lax.axis_size("tensor")
    offsets = list(range(-NEAR, NEAR + 1))
    perms = {
        d: [(i, i - d) for i in range(n_frame) if 0 <= i - d < n_frame] for d in offsets if d != 0
    }

    kv_raw = jnp.stack([k_proj, v_proj])
    first = lax.all_gather(kv_raw[:, :BLK], "frame", axis=1, tiled=False)
    tail = kv_raw[:, BLK:]
    near = {0: tail}
    for d in perms:
        near[d] = lax.ppermute(tail, "frame", perms[d])

    q_wide = q_proj.astype(jnp.float32)
    k_wide = k_proj.astype(jnp.float32)
    row_sums = lax.psum(
        (jnp.sum(q_wide * q_wide, axis=1), jnp.sum(k_wide * k_wide, axis=1)), "tensor"
    )
    q_norm = (q_wide * lax.rsqrt(row_sums[0] / full_width + EPS)[:, None] * gain_q).astype(
        jnp.bfloat16
    )
    k_sum = row_sums[1]
    all_sum = xor_gather(k_sum, n_frame, frame_pos)
    near_slab = jnp.clip(frame_pos + jnp.array(offsets), 0, n_frame - 1)
    near_sum = all_sum[near_slab][:, BLK:].reshape(len(offsets) * (blocks - 1), BLK)
    near_scale = lax.rsqrt(near_sum / full_width + EPS)[:, :, None]
    first_scale = lax.rsqrt(all_sum[:, :BLK] / full_width + EPS)[:, :, None]
    k_near = jnp.concatenate(
        [near[d][0].reshape(blocks - 1, BLK, width) for d in offsets], axis=0
    )
    kn_near = (k_near.astype(jnp.float32) * near_scale * gain_k).astype(jnp.bfloat16)
    v_near = jnp.concatenate(
        [near[d][1].reshape(blocks - 1, BLK, width) for d in offsets], axis=0
    )
    kn_first = (first[0].astype(jnp.float32) * first_scale * gain_k).astype(jnp.bfloat16)

    q_tiles = lax.dynamic_slice_in_dim(tiles, frame_pos * blocks, blocks, 0)
    key_slab = q_tiles // blocks
    within = q_tiles % blocks
    dist = key_slab - frame_pos
    near_ok = (jnp.abs(dist) <= NEAR) & (within > 0)
    near_idx = jnp.clip((dist + NEAR) * (blocks - 1) + within - 1, 0, len(offsets) * (blocks - 1) - 1)
    first_idx = jnp.clip(key_slab, 0, n_frame - 1)
    sel = jnp.stack([near_ok.astype(jnp.int32), near_idx, first_idx]).astype(jnp.int32)
    return sparse_attend(sel, q_norm, kn_near, v_near, kn_first, first)


def solution(mesh):
    return jax.shard_map(
        functools.partial(body, n_frame=mesh.shape["frame"]),
        mesh=mesh,
        in_specs=(
            P(("dp", "frame"), "tensor"),
            P(("dp", "frame"), "tensor"),
            P(("dp", "frame"), "tensor"),
            P("tensor"),
            P("tensor"),
            P("dp", None),
        ),
        out_specs=P(("dp", "frame"), "tensor"),
        check_vma=False,
    )
```

```python
import functools
import math

import jax
import jax.numpy as jnp
from jax import lax
from jax.experimental import pallas as pl
from jax.experimental.pallas import tpu as pltpu
from jax.sharding import PartitionSpec as P


HD = 128
BLK = 128
NEAR = 2

EPS = 1e-06


def attn_kernel(sel_ref, q_ref, kn_ref, vn_ref, kf_ref, vf_ref, o_ref, kc_ref, vc_ref, *, q_blocks, slots):
    scale = 1.0 / math.sqrt(HD)
    for b in range(q_blocks):
        for j in range(slots):
            use_near = sel_ref[0, b, j] == 1
            rows = pl.ds(j * BLK, BLK)
            kc_ref[rows, :] = jnp.where(use_near, kn_ref[sel_ref[1, b, j]], kf_ref[sel_ref[2, b, j]])
            vc_ref[rows, :] = jnp.where(
                use_near, vn_ref[sel_ref[1, b, j]], vf_ref[0, sel_ref[2, b, j]]
            )
        qh = q_ref[pl.ds(b * BLK, BLK), :]
        s = lax.dot_general(
            kc_ref[...], qh, (((1,), (1,)), ((), ())), preferred_element_type=jnp.float32
        ) * scale
        top = jnp.max(s, axis=0, keepdims=True)
        w = jnp.exp(s - top)
        total = jnp.sum(w, axis=0, keepdims=True)
        acc = lax.dot_general(
            w.astype(jnp.bfloat16), vc_ref[...], (((0,), (0,)), ((), ())),
            preferred_element_type=jnp.float32,
        )
        total = jnp.transpose(jnp.broadcast_to(total, (BLK, BLK)))
        o_ref[pl.ds(b * BLK, BLK), :] = (acc / total).astype(o_ref.dtype)


def sparse_attend(sel, qn, kn_near, v_near, kn_first, first):
    tok_rows, width = qn.shape
    heads = width // HD
    q_blocks = tok_rows // BLK
    slots = sel.shape[2]
    n_near = kn_near.shape[0]
    n_first = kn_first.shape[0]
    kernel = functools.partial(attn_kernel, q_blocks=q_blocks, slots=slots)
    grid_spec = pltpu.PrefetchScalarGridSpec(
        num_scalar_prefetch=1,
        grid=(heads,),
        in_specs=[
            pl.BlockSpec((tok_rows, HD), lambda h, sel_ref: (0, h)),
            pl.BlockSpec((n_near, BLK, HD), lambda h, sel_ref: (0, 0, h)),
            pl.BlockSpec((n_near, BLK, HD), lambda h, sel_ref: (0, 0, h)),
            pl.BlockSpec((n_first, BLK, HD), lambda h, sel_ref: (0, 0, h)),
            pl.BlockSpec((1, n_first, BLK, HD), lambda h, sel_ref: (1, 0, 0, h)),
        ],
        out_specs=pl.BlockSpec((tok_rows, HD), lambda h, sel_ref: (0, h)),
        scratch_shapes=[
            pltpu.VMEM((slots * BLK, HD), jnp.bfloat16),
            pltpu.VMEM((slots * BLK, HD), jnp.bfloat16),
        ],
    )
    flops = 4 * q_blocks * slots * heads * BLK * BLK * HD
    return pl.pallas_call(
        kernel,
        grid_spec=grid_spec,
        out_shape=jax.ShapeDtypeStruct((tok_rows, width), jnp.bfloat16),
        compiler_params=pltpu.CompilerParams(vmem_limit_bytes=48 * 1024 * 1024),
        cost_estimate=pl.CostEstimate(
            flops=flops,
            transcendentals=q_blocks * slots * heads * BLK * BLK,
            bytes_accessed=2 * (2 * tok_rows * width + 2 * (n_near + n_first) * BLK * width),
        ),
    )(sel, qn, kn_near, v_near, kn_first, first)


def xor_gather(piece, n_frame, frame_pos):
    held = piece[None]
    bit = 1
    while bit < n_frame:
        perm = [(i, i ^ bit) for i in range(n_frame)]
        got = lax.ppermute(held, "frame", perm)
        upper = (frame_pos // bit) % 2 == 1
        held = jnp.where(
            upper, jnp.concatenate([got, held], axis=0), jnp.concatenate([held, got], axis=0)
        )
        bit *= 2
    return held


def xor_sum(x, axis, n):
    bit = 1
    while bit < n:
        perm = [(i, i ^ bit) for i in range(n)]
        x = x + lax.ppermute(x, axis, perm)
        bit *= 2
    return x


def body(q_proj, k_proj, v_proj, gain_q, gain_k, tiles, *, n_frame, n_tensor):
    tok_rows, width = q_proj.shape
    blocks = tok_rows // BLK
    frame_pos = lax.axis_index("frame")
    full_width = width * lax.axis_size("tensor")
    offsets = list(range(-NEAR, NEAR + 1))
    perms = {
        d: [(i, i - d) for i in range(n_frame) if 0 <= i - d < n_frame] for d in offsets if d != 0
    }

    kv_raw = jnp.stack([k_proj, v_proj])
    first = lax.all_gather(kv_raw[:, :BLK], "frame", axis=1, tiled=False)
    tail = kv_raw[:, BLK:]
    near = {0: tail}
    for d in perms:
        near[d] = lax.ppermute(tail, "frame", perms[d])

    q_wide = q_proj.astype(jnp.float32)
    k_wide = k_proj.astype(jnp.float32)
    row_sums = xor_sum(
        jnp.stack([jnp.sum(q_wide * q_wide, axis=1), jnp.sum(k_wide * k_wide, axis=1)]),
        "tensor",
        n_tensor,
    )
    q_norm = (q_wide * lax.rsqrt(row_sums[0] / full_width + EPS)[:, None] * gain_q).astype(
        jnp.bfloat16
    )
    k_sum = row_sums[1]
    all_sum = xor_gather(k_sum, n_frame, frame_pos)
    near_slab = jnp.clip(frame_pos + jnp.array(offsets), 0, n_frame - 1)
    near_sum = all_sum[near_slab][:, BLK:].reshape(len(offsets) * (blocks - 1), BLK)
    near_scale = lax.rsqrt(near_sum / full_width + EPS)[:, :, None]
    first_scale = lax.rsqrt(all_sum[:, :BLK] / full_width + EPS)[:, :, None]
    k_near = jnp.concatenate(
        [near[d][0].reshape(blocks - 1, BLK, width) for d in offsets], axis=0
    )
    kn_near = (k_near.astype(jnp.float32) * near_scale * gain_k).astype(jnp.bfloat16)
    v_near = jnp.concatenate(
        [near[d][1].reshape(blocks - 1, BLK, width) for d in offsets], axis=0
    )
    kn_first = (first[0].astype(jnp.float32) * first_scale * gain_k).astype(jnp.bfloat16)

    q_tiles = lax.dynamic_slice_in_dim(tiles, frame_pos * blocks, blocks, 0)
    key_slab = q_tiles // blocks
    within = q_tiles % blocks
    dist = key_slab - frame_pos
    near_ok = (jnp.abs(dist) <= NEAR) & (within > 0)
    near_idx = jnp.clip((dist + NEAR) * (blocks - 1) + within - 1, 0, len(offsets) * (blocks - 1) - 1)
    first_idx = jnp.clip(key_slab, 0, n_frame - 1)
    sel = jnp.stack([near_ok.astype(jnp.int32), near_idx, first_idx]).astype(jnp.int32)
    return sparse_attend(sel, q_norm, kn_near, v_near, kn_first, first)


def solution(mesh):
    return jax.shard_map(
        functools.partial(body, n_frame=mesh.shape["frame"], n_tensor=mesh.shape["tensor"]),
        mesh=mesh,
        in_specs=(
            P(("dp", "frame"), "tensor"),
            P(("dp", "frame"), "tensor"),
            P(("dp", "frame"), "tensor"),
            P("tensor"),
            P("tensor"),
            P("dp", None),
        ),
        out_specs=P(("dp", "frame"), "tensor"),
        check_vma=False,
    )
```

```python
import functools
import math

import jax
import jax.numpy as jnp
from jax import lax
from jax.experimental import pallas as pl
from jax.experimental.pallas import tpu as pltpu
from jax.sharding import PartitionSpec as P


HD = 128
BLK = 128
NEAR = 2

EPS = 1e-06


def attn_kernel(
    sel_ref, q_ref, kn_ref, vn_ref, kf_ref, vf_ref, fs_ref, g_ref, o_ref, kfn_ref, kc_ref, vc_ref,
    *, q_blocks, slots,
):
    scale = 1.0 / math.sqrt(HD)
    kfn_ref[...] = (kf_ref[0].astype(jnp.float32) * fs_ref[...] * g_ref[...]).astype(jnp.bfloat16)
    for b in range(q_blocks):
        for j in range(slots):
            use_near = sel_ref[0, b, j] == 1
            rows = pl.ds(j * BLK, BLK)
            kc_ref[rows, :] = jnp.where(use_near, kn_ref[sel_ref[1, b, j]], kfn_ref[sel_ref[2, b, j]])
            vc_ref[rows, :] = jnp.where(
                use_near, vn_ref[sel_ref[1, b, j]], vf_ref[0, sel_ref[2, b, j]]
            )
        qh = q_ref[pl.ds(b * BLK, BLK), :]
        s = lax.dot_general(
            kc_ref[...], qh, (((1,), (1,)), ((), ())), preferred_element_type=jnp.float32
        ) * scale
        top = jnp.max(s, axis=0, keepdims=True)
        w = jnp.exp(s - top)
        total = jnp.sum(w, axis=0, keepdims=True)
        acc = lax.dot_general(
            w.astype(jnp.bfloat16), vc_ref[...], (((0,), (0,)), ((), ())),
            preferred_element_type=jnp.float32,
        )
        total = jnp.transpose(jnp.broadcast_to(total, (BLK, BLK)))
        o_ref[pl.ds(b * BLK, BLK), :] = (acc / total).astype(o_ref.dtype)


def sparse_attend(sel, qn, kn_near, v_near, first, first_scale, gain_k):
    tok_rows, width = qn.shape
    heads = width // HD
    q_blocks = tok_rows // BLK
    slots = sel.shape[2]
    n_near = kn_near.shape[0]
    n_first = first.shape[1]
    kernel = functools.partial(attn_kernel, q_blocks=q_blocks, slots=slots)
    grid_spec = pltpu.PrefetchScalarGridSpec(
        num_scalar_prefetch=1,
        grid=(heads,),
        in_specs=[
            pl.BlockSpec((tok_rows, HD), lambda h, sel_ref: (0, h)),
            pl.BlockSpec((n_near, BLK, HD), lambda h, sel_ref: (0, 0, h)),
            pl.BlockSpec((n_near, BLK, HD), lambda h, sel_ref: (0, 0, h)),
            pl.BlockSpec((1, n_first, BLK, HD), lambda h, sel_ref: (0, 0, 0, h)),
            pl.BlockSpec((1, n_first, BLK, HD), lambda h, sel_ref: (1, 0, 0, h)),
            pl.BlockSpec((n_first, BLK, 1), lambda h, sel_ref: (0, 0, 0)),
            pl.BlockSpec((1, HD), lambda h, sel_ref: (0, h)),
        ],
        out_specs=pl.BlockSpec((tok_rows, HD), lambda h, sel_ref: (0, h)),
        scratch_shapes=[
            pltpu.VMEM((n_first, BLK, HD), jnp.bfloat16),
            pltpu.VMEM((slots * BLK, HD), jnp.bfloat16),
            pltpu.VMEM((slots * BLK, HD), jnp.bfloat16),
        ],
    )
    flops = 4 * q_blocks * slots * heads * BLK * BLK * HD
    return pl.pallas_call(
        kernel,
        grid_spec=grid_spec,
        out_shape=jax.ShapeDtypeStruct((tok_rows, width), jnp.bfloat16),
        compiler_params=pltpu.CompilerParams(vmem_limit_bytes=48 * 1024 * 1024),
        cost_estimate=pl.CostEstimate(
            flops=flops,
            transcendentals=q_blocks * slots * heads * BLK * BLK,
            bytes_accessed=2 * (2 * tok_rows * width + 2 * (n_near + n_first) * BLK * width),
        ),
    )(sel, qn, kn_near, v_near, first, first, first_scale, gain_k.reshape(1, width))


def xor_gather(piece, n_frame, frame_pos):
    held = piece[None]
    bit = 1
    while bit < n_frame:
        perm = [(i, i ^ bit) for i in range(n_frame)]
        got = lax.ppermute(held, "frame", perm)
        upper = (frame_pos // bit) % 2 == 1
        held = jnp.where(
            upper, jnp.concatenate([got, held], axis=0), jnp.concatenate([held, got], axis=0)
        )
        bit *= 2
    return held


def xor_sum(x, axis, n):
    bit = 1
    while bit < n:
        perm = [(i, i ^ bit) for i in range(n)]
        x = x + lax.ppermute(x, axis, perm)
        bit *= 2
    return x


def body(q_proj, k_proj, v_proj, gain_q, gain_k, tiles, *, n_frame, n_tensor):
    tok_rows, width = q_proj.shape
    blocks = tok_rows // BLK
    frame_pos = lax.axis_index("frame")
    full_width = width * lax.axis_size("tensor")
    offsets = list(range(-NEAR, NEAR + 1))
    perms = {
        d: [(i, i - d) for i in range(n_frame) if 0 <= i - d < n_frame] for d in offsets if d != 0
    }

    kv_raw = jnp.stack([k_proj, v_proj])
    first = lax.all_gather(kv_raw[:, :BLK], "frame", axis=1, tiled=False)
    tail = kv_raw[:, BLK:]
    near = {0: tail}
    for d in perms:
        near[d] = lax.ppermute(tail, "frame", perms[d])

    q_wide = q_proj.astype(jnp.float32)
    k_wide = k_proj.astype(jnp.float32)
    row_sums = xor_sum(
        jnp.stack([jnp.sum(q_wide * q_wide, axis=1), jnp.sum(k_wide * k_wide, axis=1)]),
        "tensor",
        n_tensor,
    )
    q_norm = (q_wide * lax.rsqrt(row_sums[0] / full_width + EPS)[:, None] * gain_q).astype(
        jnp.bfloat16
    )
    k_sum = row_sums[1]
    all_sum = xor_gather(k_sum, n_frame, frame_pos)
    near_slab = jnp.clip(frame_pos + jnp.array(offsets), 0, n_frame - 1)
    near_sum = all_sum[near_slab][:, BLK:].reshape(len(offsets) * (blocks - 1), BLK)
    near_scale = lax.rsqrt(near_sum / full_width + EPS)[:, :, None]
    first_scale = lax.rsqrt(all_sum[:, :BLK] / full_width + EPS)[:, :, None]
    k_near = jnp.concatenate(
        [near[d][0].reshape(blocks - 1, BLK, width) for d in offsets], axis=0
    )
    kn_near = (k_near.astype(jnp.float32) * near_scale * gain_k).astype(jnp.bfloat16)
    v_near = jnp.concatenate(
        [near[d][1].reshape(blocks - 1, BLK, width) for d in offsets], axis=0
    )

    q_tiles = lax.dynamic_slice_in_dim(tiles, frame_pos * blocks, blocks, 0)
    key_slab = q_tiles // blocks
    within = q_tiles % blocks
    dist = key_slab - frame_pos
    near_ok = (jnp.abs(dist) <= NEAR) & (within > 0)
    near_idx = jnp.clip((dist + NEAR) * (blocks - 1) + within - 1, 0, len(offsets) * (blocks - 1) - 1)
    first_idx = jnp.clip(key_slab, 0, n_frame - 1)
    sel = jnp.stack([near_ok.astype(jnp.int32), near_idx, first_idx]).astype(jnp.int32)
    return sparse_attend(sel, q_norm, kn_near, v_near, first, first_scale, gain_k)


def solution(mesh):
    return jax.shard_map(
        functools.partial(body, n_frame=mesh.shape["frame"], n_tensor=mesh.shape["tensor"]),
        mesh=mesh,
        in_specs=(
            P(("dp", "frame"), "tensor"),
            P(("dp", "frame"), "tensor"),
            P(("dp", "frame"), "tensor"),
            P("tensor"),
            P("tensor"),
            P("dp", None),
        ),
        out_specs=P(("dp", "frame"), "tensor"),
        check_vma=False,
    )
```

```python
import functools
import math

import jax
import jax.numpy as jnp
from jax import lax
from jax.experimental import pallas as pl
from jax.experimental.pallas import tpu as pltpu
from jax.sharding import PartitionSpec as P


HD = 128
BLK = 128
NEAR = 2

EPS = 1e-06
FRAME = ("zl", "y")
Y_SIZE = 4


def attn_kernel(sel_ref, q_ref, kn_ref, vn_ref, kf_ref, vf_ref, o_ref, kc_ref, vc_ref, *, q_blocks, slots):
    scale = 1.0 / math.sqrt(HD)
    for b in range(q_blocks):
        for j in range(slots):
            use_near = sel_ref[0, b, j] == 1
            rows = pl.ds(j * BLK, BLK)
            kc_ref[rows, :] = jnp.where(use_near, kn_ref[sel_ref[1, b, j]], kf_ref[sel_ref[2, b, j]])
            vc_ref[rows, :] = jnp.where(
                use_near, vn_ref[sel_ref[1, b, j]], vf_ref[0, sel_ref[2, b, j]]
            )
        qh = q_ref[pl.ds(b * BLK, BLK), :]
        s = lax.dot_general(
            kc_ref[...], qh, (((1,), (1,)), ((), ())), preferred_element_type=jnp.float32
        ) * scale
        top = jnp.max(s, axis=0, keepdims=True)
        w = jnp.exp(s - top)
        total = jnp.sum(w, axis=0, keepdims=True)
        acc = lax.dot_general(
            w.astype(jnp.bfloat16), vc_ref[...], (((0,), (0,)), ((), ())),
            preferred_element_type=jnp.float32,
        )
        total = jnp.transpose(jnp.broadcast_to(total, (BLK, BLK)))
        o_ref[pl.ds(b * BLK, BLK), :] = (acc / total).astype(o_ref.dtype)


def sparse_attend(sel, qn, kn_near, v_near, kn_first, first):
    tok_rows, width = qn.shape
    heads = width // HD
    q_blocks = tok_rows // BLK
    slots = sel.shape[2]
    n_near = kn_near.shape[0]
    n_first = kn_first.shape[0]
    kernel = functools.partial(attn_kernel, q_blocks=q_blocks, slots=slots)
    grid_spec = pltpu.PrefetchScalarGridSpec(
        num_scalar_prefetch=1,
        grid=(heads,),
        in_specs=[
            pl.BlockSpec((tok_rows, HD), lambda h, sel_ref: (0, h)),
            pl.BlockSpec((n_near, BLK, HD), lambda h, sel_ref: (0, 0, h)),
            pl.BlockSpec((n_near, BLK, HD), lambda h, sel_ref: (0, 0, h)),
            pl.BlockSpec((n_first, BLK, HD), lambda h, sel_ref: (0, 0, h)),
            pl.BlockSpec((1, n_first, BLK, HD), lambda h, sel_ref: (1, 0, 0, h)),
        ],
        out_specs=pl.BlockSpec((tok_rows, HD), lambda h, sel_ref: (0, h)),
        scratch_shapes=[
            pltpu.VMEM((slots * BLK, HD), jnp.bfloat16),
            pltpu.VMEM((slots * BLK, HD), jnp.bfloat16),
        ],
    )
    flops = 4 * q_blocks * slots * heads * BLK * BLK * HD
    return pl.pallas_call(
        kernel,
        grid_spec=grid_spec,
        out_shape=jax.ShapeDtypeStruct((tok_rows, width), jnp.bfloat16),
        compiler_params=pltpu.CompilerParams(vmem_limit_bytes=48 * 1024 * 1024),
        cost_estimate=pl.CostEstimate(
            flops=flops,
            transcendentals=q_blocks * slots * heads * BLK * BLK,
            bytes_accessed=2 * (2 * tok_rows * width + 2 * (n_near + n_first) * BLK * width),
        ),
    )(sel, qn, kn_near, v_near, kn_first, first)


def xor_gather(piece, n_frame, frame_pos):
    held = piece[None]
    bit = 1
    while bit < n_frame:
        perm = [(i, i ^ bit) for i in range(n_frame)]
        got = lax.ppermute(held, FRAME, perm)
        upper = (frame_pos // bit) % 2 == 1
        held = jnp.where(
            upper, jnp.concatenate([got, held], axis=0), jnp.concatenate([held, got], axis=0)
        )
        bit *= 2
    return held


def xor_sum(x, axis, n):
    bit = 1
    while bit < n:
        perm = [(i, i ^ bit) for i in range(n)]
        x = x + lax.ppermute(x, axis, perm)
        bit *= 2
    return x


def body(q_proj, k_proj, v_proj, gain_q, gain_k, tiles, *, n_frame, n_tensor):
    tok_rows, width = q_proj.shape
    blocks = tok_rows // BLK
    frame_pos = lax.axis_index("zl") * lax.axis_size("y") + lax.axis_index("y")
    full_width = width * lax.axis_size("tensor")
    offsets = list(range(-NEAR, NEAR + 1))
    perms = {
        d: [(i, i - d) for i in range(n_frame) if 0 <= i - d < n_frame] for d in offsets if d != 0
    }

    kv_raw = jnp.stack([k_proj, v_proj])
    first = lax.all_gather(kv_raw[:, :BLK], "y", axis=1, tiled=False)
    first = lax.all_gather(first, "zl", axis=1, tiled=False)
    first = first.reshape(2, n_frame, BLK, width)
    tail = kv_raw[:, BLK:]
    near = {0: tail}
    for d in perms:
        near[d] = lax.ppermute(tail, FRAME, perms[d])

    q_wide = q_proj.astype(jnp.float32)
    k_wide = k_proj.astype(jnp.float32)
    row_sums = xor_sum(
        jnp.stack([jnp.sum(q_wide * q_wide, axis=1), jnp.sum(k_wide * k_wide, axis=1)]),
        "tensor",
        n_tensor,
    )
    q_norm = (q_wide * lax.rsqrt(row_sums[0] / full_width + EPS)[:, None] * gain_q).astype(
        jnp.bfloat16
    )
    k_sum = row_sums[1]
    all_sum = xor_gather(k_sum, n_frame, frame_pos)
    near_slab = jnp.clip(frame_pos + jnp.array(offsets), 0, n_frame - 1)
    near_sum = all_sum[near_slab][:, BLK:].reshape(len(offsets) * (blocks - 1), BLK)
    near_scale = lax.rsqrt(near_sum / full_width + EPS)[:, :, None]
    first_scale = lax.rsqrt(all_sum[:, :BLK] / full_width + EPS)[:, :, None]
    k_near = jnp.concatenate(
        [near[d][0].reshape(blocks - 1, BLK, width) for d in offsets], axis=0
    )
    kn_near = (k_near.astype(jnp.float32) * near_scale * gain_k).astype(jnp.bfloat16)
    v_near = jnp.concatenate(
        [near[d][1].reshape(blocks - 1, BLK, width) for d in offsets], axis=0
    )
    kn_first = (first[0].astype(jnp.float32) * first_scale * gain_k).astype(jnp.bfloat16)

    q_tiles = lax.dynamic_slice_in_dim(tiles, frame_pos * blocks, blocks, 0)
    key_slab = q_tiles // blocks
    within = q_tiles % blocks
    dist = key_slab - frame_pos
    near_ok = (jnp.abs(dist) <= NEAR) & (within > 0)
    near_idx = jnp.clip((dist + NEAR) * (blocks - 1) + within - 1, 0, len(offsets) * (blocks - 1) - 1)
    first_idx = jnp.clip(key_slab, 0, n_frame - 1)
    sel = jnp.stack([near_ok.astype(jnp.int32), near_idx, first_idx]).astype(jnp.int32)
    return sparse_attend(sel, q_norm, kn_near, v_near, kn_first, first)


def solution(mesh):
    n_frame, n_tensor, n_dp = (mesh.shape[a] for a in ("frame", "tensor", "dp"))
    assert mesh.axis_names == ("frame", "tensor", "dp") and n_frame % Y_SIZE == 0
    split = jax.sharding.Mesh(
        mesh.devices.reshape(n_frame // Y_SIZE, Y_SIZE, n_tensor, n_dp), ("zl", "y", "tensor", "dp")
    )
    return jax.shard_map(
        functools.partial(body, n_frame=mesh.shape["frame"], n_tensor=mesh.shape["tensor"]),
        mesh=split,
        in_specs=(
            P(("dp", "zl", "y"), "tensor"),
            P(("dp", "zl", "y"), "tensor"),
            P(("dp", "zl", "y"), "tensor"),
            P("tensor"),
            P("tensor"),
            P("dp", None),
        ),
        out_specs=P(("dp", "zl", "y"), "tensor"),
        check_vma=False,
    )
```

```python
import functools
import math

import jax
import jax.numpy as jnp
from jax import lax
from jax.experimental import pallas as pl
from jax.experimental.pallas import tpu as pltpu
from jax.sharding import PartitionSpec as P


HD = 128
BLK = 128
NEAR = 2

EPS = 1e-06
LOG2E = 1.4426950408889634


def attn_kernel(sel_ref, q_ref, kn_ref, vn_ref, kf_ref, vf_ref, o_ref, kc_ref, vc_ref, *, q_blocks, slots):
    scale = 1.0 / math.sqrt(HD)
    cols = pl.ds(pl.multiple_of(pl.program_id(0) * HD, HD), HD)
    for b in range(q_blocks):
        for j in range(slots):
            use_near = sel_ref[0, b, j] == 1
            rows = pl.ds(j * BLK, BLK)
            kc_ref[rows, :] = jnp.where(
                use_near, kn_ref[sel_ref[1, b, j], :, cols], kf_ref[sel_ref[2, b, j]]
            )
            vc_ref[rows, :] = jnp.where(
                use_near, vn_ref[sel_ref[1, b, j], :, cols], vf_ref[0, sel_ref[2, b, j]]
            )
        qh = q_ref[pl.ds(b * BLK, BLK), :]
        s = lax.dot_general(
            kc_ref[...], qh, (((1,), (1,)), ((), ())), preferred_element_type=jnp.float32
        ) * scale
        top = jnp.max(s, axis=0, keepdims=True)
        w = jnp.exp2((s - top) * LOG2E)
        total = jnp.sum(w, axis=0, keepdims=True)
        acc = lax.dot_general(
            w.astype(jnp.bfloat16), vc_ref[...], (((0,), (0,)), ((), ())),
            preferred_element_type=jnp.float32,
        )
        total = jnp.transpose(jnp.broadcast_to(total, (BLK, BLK)))
        o_ref[pl.ds(b * BLK, BLK), :] = (acc / total).astype(o_ref.dtype)


def sparse_attend(sel, qn, kn_near, v_near, kn_first, first):
    tok_rows, width = qn.shape
    heads = width // HD
    q_blocks = tok_rows // BLK
    slots = sel.shape[2]
    n_near = kn_near.shape[0]
    n_first = kn_first.shape[0]
    kernel = functools.partial(attn_kernel, q_blocks=q_blocks, slots=slots)
    grid_spec = pltpu.PrefetchScalarGridSpec(
        num_scalar_prefetch=1,
        grid=(heads,),
        in_specs=[
            pl.BlockSpec((tok_rows, HD), lambda h, sel_ref: (0, h)),
            pl.BlockSpec(memory_space=pltpu.VMEM),
            pl.BlockSpec(memory_space=pltpu.VMEM),
            pl.BlockSpec((n_first, BLK, HD), lambda h, sel_ref: (0, 0, h)),
            pl.BlockSpec((1, n_first, BLK, HD), lambda h, sel_ref: (1, 0, 0, h)),
        ],
        out_specs=pl.BlockSpec((tok_rows, HD), lambda h, sel_ref: (0, h)),
        scratch_shapes=[
            pltpu.VMEM((slots * BLK, HD), jnp.bfloat16),
            pltpu.VMEM((slots * BLK, HD), jnp.bfloat16),
        ],
    )
    flops = 4 * q_blocks * slots * heads * BLK * BLK * HD
    return pl.pallas_call(
        kernel,
        grid_spec=grid_spec,
        out_shape=jax.ShapeDtypeStruct((tok_rows, width), jnp.bfloat16),
        compiler_params=pltpu.CompilerParams(vmem_limit_bytes=48 * 1024 * 1024),
        cost_estimate=pl.CostEstimate(
            flops=flops,
            transcendentals=q_blocks * slots * heads * BLK * BLK,
            bytes_accessed=2 * (2 * tok_rows * width + 2 * (n_near + n_first) * BLK * width),
        ),
    )(sel, qn, kn_near, v_near, kn_first, first)


def xor_gather(piece, n_frame, frame_pos):
    held = piece[None]
    bit = 1
    while bit < n_frame:
        perm = [(i, i ^ bit) for i in range(n_frame)]
        got = lax.ppermute(held, "frame", perm)
        upper = (frame_pos // bit) % 2 == 1
        held = jnp.where(
            upper, jnp.concatenate([got, held], axis=0), jnp.concatenate([held, got], axis=0)
        )
        bit *= 2
    return held


def xor_sum(x, axis, n):
    bit = 1
    while bit < n:
        perm = [(i, i ^ bit) for i in range(n)]
        x = x + lax.ppermute(x, axis, perm)
        bit *= 2
    return x


def body(q_proj, k_proj, v_proj, gain_q, gain_k, tiles, *, n_frame, n_tensor):
    tok_rows, width = q_proj.shape
    blocks = tok_rows // BLK
    frame_pos = lax.axis_index("frame")
    full_width = width * lax.axis_size("tensor")
    offsets = list(range(-NEAR, NEAR + 1))
    perms = {
        d: [(i, i - d) for i in range(n_frame) if 0 <= i - d < n_frame] for d in offsets if d != 0
    }

    kv_raw = jnp.stack([k_proj, v_proj])
    first = lax.all_gather(kv_raw[:, :BLK], "frame", axis=1, tiled=False)
    tail = kv_raw[:, BLK:]
    near = {0: tail}
    for d in perms:
        near[d] = lax.ppermute(tail, "frame", perms[d])

    q_wide = q_proj.astype(jnp.float32)
    k_wide = k_proj.astype(jnp.float32)
    row_sums = xor_sum(
        jnp.stack([jnp.sum(q_wide * q_wide, axis=1), jnp.sum(k_wide * k_wide, axis=1)]),
        "tensor",
        n_tensor,
    )
    q_norm = (q_wide * lax.rsqrt(row_sums[0] / full_width + EPS)[:, None] * gain_q).astype(
        jnp.bfloat16
    )
    k_sum = row_sums[1]
    all_sum = xor_gather(k_sum, n_frame, frame_pos)
    near_slab = jnp.clip(frame_pos + jnp.array(offsets), 0, n_frame - 1)
    near_sum = all_sum[near_slab][:, BLK:].reshape(len(offsets) * (blocks - 1), BLK)
    near_scale = lax.rsqrt(near_sum / full_width + EPS)[:, :, None]
    first_scale = lax.rsqrt(all_sum[:, :BLK] / full_width + EPS)[:, :, None]
    k_near = jnp.concatenate(
        [near[d][0].reshape(blocks - 1, BLK, width) for d in offsets], axis=0
    )
    kn_near = (k_near.astype(jnp.float32) * near_scale * gain_k).astype(jnp.bfloat16)
    v_near = jnp.concatenate(
        [near[d][1].reshape(blocks - 1, BLK, width) for d in offsets], axis=0
    )
    kn_first = (first[0].astype(jnp.float32) * first_scale * gain_k).astype(jnp.bfloat16)

    q_tiles = lax.dynamic_slice_in_dim(tiles, frame_pos * blocks, blocks, 0)
    key_slab = q_tiles // blocks
    within = q_tiles % blocks
    dist = key_slab - frame_pos
    near_ok = (jnp.abs(dist) <= NEAR) & (within > 0)
    near_idx = jnp.clip((dist + NEAR) * (blocks - 1) + within - 1, 0, len(offsets) * (blocks - 1) - 1)
    first_idx = jnp.clip(key_slab, 0, n_frame - 1)
    sel = jnp.stack([near_ok.astype(jnp.int32), near_idx, first_idx]).astype(jnp.int32)
    return sparse_attend(sel, q_norm, kn_near, v_near, kn_first, first)


def solution(mesh):
    return jax.shard_map(
        functools.partial(body, n_frame=mesh.shape["frame"], n_tensor=mesh.shape["tensor"]),
        mesh=mesh,
        in_specs=(
            P(("dp", "frame"), "tensor"),
            P(("dp", "frame"), "tensor"),
            P(("dp", "frame"), "tensor"),
            P("tensor"),
            P("tensor"),
            P("dp", None),
        ),
        out_specs=P(("dp", "frame"), "tensor"),
        check_vma=False,
    )
```

```python
import functools
import math

import jax
import jax.numpy as jnp
from jax import lax
from jax.experimental import pallas as pl
from jax.experimental.pallas import tpu as pltpu
from jax.sharding import PartitionSpec as P


HD = 128
BLK = 128
NEAR = 2

EPS = 1e-06


def attn_kernel(sel_ref, q_ref, kn_ref, vn_ref, kf_ref, vf_ref, o_ref, kc_ref, vc_ref, *, q_blocks, slots):
    scale = 1.0 / math.sqrt(HD)
    cols = pl.ds(pl.multiple_of(pl.program_id(0) * HD, HD), HD)
    for b in range(q_blocks):
        for j in range(slots):
            use_near = sel_ref[0, b, j] == 1
            rows = pl.ds(j * BLK, BLK)
            kc_ref[rows, :] = jnp.where(
                use_near, kn_ref[sel_ref[1, b, j], :, cols], kf_ref[sel_ref[2, b, j]]
            )
            vc_ref[rows, :] = jnp.where(
                use_near, vn_ref[sel_ref[1, b, j], :, cols], vf_ref[sel_ref[2, b, j], 0]
            )
        qh = q_ref[pl.ds(b * BLK, BLK), :]
        s = lax.dot_general(
            kc_ref[...], qh, (((1,), (1,)), ((), ())), preferred_element_type=jnp.float32
        ) * scale
        top = jnp.max(s, axis=0, keepdims=True)
        w = jnp.exp(s - top)
        total = jnp.sum(w, axis=0, keepdims=True)
        acc = lax.dot_general(
            w.astype(jnp.bfloat16), vc_ref[...], (((0,), (0,)), ((), ())),
            preferred_element_type=jnp.float32,
        )
        total = jnp.transpose(jnp.broadcast_to(total, (BLK, BLK)))
        o_ref[pl.ds(b * BLK, BLK), :] = (acc / total).astype(o_ref.dtype)


def sparse_attend(sel, qn, kn_near, v_near, kn_first, first):
    tok_rows, width = qn.shape
    heads = width // HD
    q_blocks = tok_rows // BLK
    slots = sel.shape[2]
    n_near = kn_near.shape[0]
    n_first = kn_first.shape[0]
    kernel = functools.partial(attn_kernel, q_blocks=q_blocks, slots=slots)
    grid_spec = pltpu.PrefetchScalarGridSpec(
        num_scalar_prefetch=1,
        grid=(heads,),
        in_specs=[
            pl.BlockSpec((tok_rows, HD), lambda h, sel_ref: (0, h)),
            pl.BlockSpec(memory_space=pltpu.VMEM),
            pl.BlockSpec(memory_space=pltpu.VMEM),
            pl.BlockSpec((n_first, BLK, HD), lambda h, sel_ref: (0, 0, h)),
            pl.BlockSpec((n_first, 1, BLK, HD), lambda h, sel_ref: (0, 1, 0, h)),
        ],
        out_specs=pl.BlockSpec((tok_rows, HD), lambda h, sel_ref: (0, h)),
        scratch_shapes=[
            pltpu.VMEM((slots * BLK, HD), jnp.bfloat16),
            pltpu.VMEM((slots * BLK, HD), jnp.bfloat16),
        ],
    )
    flops = 4 * q_blocks * slots * heads * BLK * BLK * HD
    return pl.pallas_call(
        kernel,
        grid_spec=grid_spec,
        out_shape=jax.ShapeDtypeStruct((tok_rows, width), jnp.bfloat16),
        compiler_params=pltpu.CompilerParams(vmem_limit_bytes=48 * 1024 * 1024),
        cost_estimate=pl.CostEstimate(
            flops=flops,
            transcendentals=q_blocks * slots * heads * BLK * BLK,
            bytes_accessed=2 * (2 * tok_rows * width + 2 * (n_near + n_first) * BLK * width),
        ),
    )(sel, qn, kn_near, v_near, kn_first, first)


def xor_gather(piece, n_frame, frame_pos):
    held = piece[None]
    bit = 1
    while bit < n_frame:
        perm = [(i, i ^ bit) for i in range(n_frame)]
        got = lax.ppermute(held, "frame", perm)
        upper = (frame_pos // bit) % 2 == 1
        held = jnp.where(
            upper, jnp.concatenate([got, held], axis=0), jnp.concatenate([held, got], axis=0)
        )
        bit *= 2
    return held


def xor_sum(x, axis, n):
    bit = 1
    while bit < n:
        perm = [(i, i ^ bit) for i in range(n)]
        x = x + lax.ppermute(x, axis, perm)
        bit *= 2
    return x


def body(q_proj, k_proj, v_proj, gain_q, gain_k, tiles, *, n_frame, n_tensor):
    tok_rows, width = q_proj.shape
    blocks = tok_rows // BLK
    frame_pos = lax.axis_index("frame")
    full_width = width * lax.axis_size("tensor")
    offsets = list(range(-NEAR, NEAR + 1))
    perms = {
        d: [(i, i - d) for i in range(n_frame) if 0 <= i - d < n_frame] for d in offsets if d != 0
    }

    kv_first = jnp.concatenate([k_proj[:BLK], v_proj[:BLK]], axis=0)
    first = lax.all_gather(kv_first, "frame", axis=0, tiled=False)
    first = first.reshape(n_frame, 2, BLK, width)
    tail = jnp.stack([k_proj[BLK:], v_proj[BLK:]])
    near = {0: tail}
    for d in perms:
        near[d] = lax.ppermute(tail, "frame", perms[d])

    q_wide = q_proj.astype(jnp.float32)
    k_wide = k_proj.astype(jnp.float32)
    row_sums = xor_sum(
        jnp.stack([jnp.sum(q_wide * q_wide, axis=1), jnp.sum(k_wide * k_wide, axis=1)]),
        "tensor",
        n_tensor,
    )
    q_norm = (q_wide * lax.rsqrt(row_sums[0] / full_width + EPS)[:, None] * gain_q).astype(
        jnp.bfloat16
    )
    k_sum = row_sums[1]
    all_sum = xor_gather(k_sum, n_frame, frame_pos)
    near_slab = jnp.clip(frame_pos + jnp.array(offsets), 0, n_frame - 1)
    near_sum = all_sum[near_slab][:, BLK:].reshape(len(offsets) * (blocks - 1), BLK)
    near_scale = lax.rsqrt(near_sum / full_width + EPS)[:, :, None]
    first_scale = lax.rsqrt(all_sum[:, :BLK] / full_width + EPS)[:, :, None]
    k_near = jnp.concatenate(
        [near[d][0].reshape(blocks - 1, BLK, width) for d in offsets], axis=0
    )
    kn_near = (k_near.astype(jnp.float32) * near_scale * gain_k).astype(jnp.bfloat16)
    v_near = jnp.concatenate(
        [near[d][1].reshape(blocks - 1, BLK, width) for d in offsets], axis=0
    )
    kn_first = (first[:, 0].astype(jnp.float32) * first_scale * gain_k).astype(jnp.bfloat16)

    q_tiles = lax.dynamic_slice_in_dim(tiles, frame_pos * blocks, blocks, 0)
    key_slab = q_tiles // blocks
    within = q_tiles % blocks
    dist = key_slab - frame_pos
    near_ok = (jnp.abs(dist) <= NEAR) & (within > 0)
    near_idx = jnp.clip((dist + NEAR) * (blocks - 1) + within - 1, 0, len(offsets) * (blocks - 1) - 1)
    first_idx = jnp.clip(key_slab, 0, n_frame - 1)
    sel = jnp.stack([near_ok.astype(jnp.int32), near_idx, first_idx]).astype(jnp.int32)
    return sparse_attend(sel, q_norm, kn_near, v_near, kn_first, first)


def solution(mesh):
    return jax.shard_map(
        functools.partial(body, n_frame=mesh.shape["frame"], n_tensor=mesh.shape["tensor"]),
        mesh=mesh,
        in_specs=(
            P(("dp", "frame"), "tensor"),
            P(("dp", "frame"), "tensor"),
            P(("dp", "frame"), "tensor"),
            P("tensor"),
            P("tensor"),
            P("dp", None),
        ),
        out_specs=P(("dp", "frame"), "tensor"),
        check_vma=False,
    )
```

```python
import functools
import math

import jax
import jax.numpy as jnp
from jax import lax
from jax.experimental import pallas as pl
from jax.experimental.pallas import tpu as pltpu
from jax.sharding import PartitionSpec as P


HD = 128
BLK = 128
NEAR = 2

EPS = 1e-06


def attn_kernel(sel_ref, q_ref, kn_ref, vn_ref, kf_ref, vf_ref, o_ref, kc_ref, vc_ref, *, q_blocks, slots):
    scale = 1.0 / math.sqrt(HD)
    cols = pl.ds(pl.multiple_of(pl.program_id(0) * HD, HD), HD)
    for b in range(q_blocks):
        for j in range(slots):
            use_near = sel_ref[0, b, j] == 1
            rows = pl.ds(j * BLK, BLK)
            ni = sel_ref[1, b, j]
            fi = sel_ref[2, b, j]

            @pl.when(use_near)
            def _():
                kc_ref[rows, :] = kn_ref[ni, :, cols]
                vc_ref[rows, :] = vn_ref[ni, :, cols]

            @pl.when(jnp.logical_not(use_near))
            def _():
                kc_ref[rows, :] = kf_ref[fi, :, cols]
                vc_ref[rows, :] = vf_ref[0, fi]

        qh = q_ref[pl.ds(b * BLK, BLK), :]
        s = lax.dot_general(
            kc_ref[...], qh, (((1,), (1,)), ((), ())), preferred_element_type=jnp.float32
        ) * scale
        top = jnp.max(s, axis=0, keepdims=True)
        w = jnp.exp(s - top)
        total = jnp.sum(w, axis=0, keepdims=True)
        acc = lax.dot_general(
            w.astype(jnp.bfloat16), vc_ref[...], (((0,), (0,)), ((), ())),
            preferred_element_type=jnp.float32,
        )
        total = jnp.transpose(jnp.broadcast_to(total, (BLK, BLK)))
        o_ref[pl.ds(b * BLK, BLK), :] = (acc / total).astype(o_ref.dtype)


def sparse_attend(sel, qn, kn_near, v_near, kn_first, first):
    tok_rows, width = qn.shape
    heads = width // HD
    q_blocks = tok_rows // BLK
    slots = sel.shape[2]
    n_near = kn_near.shape[0]
    n_first = kn_first.shape[0]
    kernel = functools.partial(attn_kernel, q_blocks=q_blocks, slots=slots)
    grid_spec = pltpu.PrefetchScalarGridSpec(
        num_scalar_prefetch=1,
        grid=(heads,),
        in_specs=[
            pl.BlockSpec((tok_rows, HD), lambda h, sel_ref: (0, h)),
            pl.BlockSpec(memory_space=pltpu.VMEM),
            pl.BlockSpec(memory_space=pltpu.VMEM),
            pl.BlockSpec(memory_space=pltpu.VMEM),
            pl.BlockSpec((1, n_first, BLK, HD), lambda h, sel_ref: (1, 0, 0, h)),
        ],
        out_specs=pl.BlockSpec((tok_rows, HD), lambda h, sel_ref: (0, h)),
        scratch_shapes=[
            pltpu.VMEM((slots * BLK, HD), jnp.bfloat16),
            pltpu.VMEM((slots * BLK, HD), jnp.bfloat16),
        ],
    )
    flops = 4 * q_blocks * slots * heads * BLK * BLK * HD
    return pl.pallas_call(
        kernel,
        grid_spec=grid_spec,
        out_shape=jax.ShapeDtypeStruct((tok_rows, width), jnp.bfloat16),
        compiler_params=pltpu.CompilerParams(vmem_limit_bytes=48 * 1024 * 1024),
        cost_estimate=pl.CostEstimate(
            flops=flops,
            transcendentals=q_blocks * slots * heads * BLK * BLK,
            bytes_accessed=2 * (2 * tok_rows * width + 2 * (n_near + n_first) * BLK * width),
        ),
    )(sel, qn, kn_near, v_near, kn_first, first)


def xor_gather(piece, n_frame, frame_pos):
    held = piece[None]
    bit = 1
    while bit < n_frame:
        perm = [(i, i ^ bit) for i in range(n_frame)]
        got = lax.ppermute(held, "frame", perm)
        upper = (frame_pos // bit) % 2 == 1
        held = jnp.where(
            upper, jnp.concatenate([got, held], axis=0), jnp.concatenate([held, got], axis=0)
        )
        bit *= 2
    return held


def xor_sum(x, axis, n):
    bit = 1
    while bit < n:
        perm = [(i, i ^ bit) for i in range(n)]
        x = x + lax.ppermute(x, axis, perm)
        bit *= 2
    return x


def body(q_proj, k_proj, v_proj, gain_q, gain_k, tiles, *, n_frame, n_tensor):
    tok_rows, width = q_proj.shape
    blocks = tok_rows // BLK
    frame_pos = lax.axis_index("frame")
    full_width = width * lax.axis_size("tensor")
    offsets = list(range(-NEAR, NEAR + 1))
    perms = {
        d: [(i, i - d) for i in range(n_frame) if 0 <= i - d < n_frame] for d in offsets if d != 0
    }

    kv_raw = jnp.stack([k_proj, v_proj])
    first = lax.all_gather(kv_raw[:, :BLK], "frame", axis=1, tiled=False)
    tail = kv_raw[:, BLK:]
    near = {0: tail}
    for d in perms:
        near[d] = lax.ppermute(tail, "frame", perms[d])

    q_wide = q_proj.astype(jnp.float32)
    k_wide = k_proj.astype(jnp.float32)
    row_sums = xor_sum(
        jnp.stack([jnp.sum(q_wide * q_wide, axis=1), jnp.sum(k_wide * k_wide, axis=1)]),
        "tensor",
        n_tensor,
    )
    q_norm = (q_wide * lax.rsqrt(row_sums[0] / full_width + EPS)[:, None] * gain_q).astype(
        jnp.bfloat16
    )
    k_sum = row_sums[1]
    all_sum = xor_gather(k_sum, n_frame, frame_pos)
    near_slab = jnp.clip(frame_pos + jnp.array(offsets), 0, n_frame - 1)
    near_sum = all_sum[near_slab][:, BLK:].reshape(len(offsets) * (blocks - 1), BLK)
    near_scale = lax.rsqrt(near_sum / full_width + EPS)[:, :, None]
    first_scale = lax.rsqrt(all_sum[:, :BLK] / full_width + EPS)[:, :, None]
    k_near = jnp.concatenate(
        [near[d][0].reshape(blocks - 1, BLK, width) for d in offsets], axis=0
    )
    kn_near = (k_near.astype(jnp.float32) * near_scale * gain_k).astype(jnp.bfloat16)
    v_near = jnp.concatenate(
        [near[d][1].reshape(blocks - 1, BLK, width) for d in offsets], axis=0
    )
    kn_first = (first[0].astype(jnp.float32) * first_scale * gain_k).astype(jnp.bfloat16)

    q_tiles = lax.dynamic_slice_in_dim(tiles, frame_pos * blocks, blocks, 0)
    key_slab = q_tiles // blocks
    within = q_tiles % blocks
    dist = key_slab - frame_pos
    near_ok = (jnp.abs(dist) <= NEAR) & (within > 0)
    near_idx = jnp.clip((dist + NEAR) * (blocks - 1) + within - 1, 0, len(offsets) * (blocks - 1) - 1)
    first_idx = jnp.clip(key_slab, 0, n_frame - 1)
    sel = jnp.stack([near_ok.astype(jnp.int32), near_idx, first_idx]).astype(jnp.int32)
    return sparse_attend(sel, q_norm, kn_near, v_near, kn_first, first)


def solution(mesh):
    return jax.shard_map(
        functools.partial(body, n_frame=mesh.shape["frame"], n_tensor=mesh.shape["tensor"]),
        mesh=mesh,
        in_specs=(
            P(("dp", "frame"), "tensor"),
            P(("dp", "frame"), "tensor"),
            P(("dp", "frame"), "tensor"),
            P("tensor"),
            P("tensor"),
            P("dp", None),
        ),
        out_specs=P(("dp", "frame"), "tensor"),
        check_vma=False,
    )
```

```python
import functools
import math

import jax
import jax.numpy as jnp
from jax import lax
from jax.experimental import pallas as pl
from jax.experimental.pallas import tpu as pltpu
from jax.sharding import PartitionSpec as P


HD = 128
BLK = 128
NEAR = 2

EPS = 1e-06


def attn_kernel(
    sel_ref, q_ref, kn_ref, vn_ref, kf_ref, vf_ref, o_ref, kc_ref, vc_ref, kb_ref, vb_ref,
    *, q_blocks, slots,
):
    scale = 1.0 / math.sqrt(HD)
    cols = pl.ds(pl.multiple_of(pl.program_id(0) * HD, HD), HD)
    n_near = kn_ref.shape[0]
    n_first = kf_ref.shape[0]
    kb_ref[pl.ds(0, n_near)] = kn_ref[:, :, cols]
    vb_ref[pl.ds(0, n_near)] = vn_ref[:, :, cols]
    kb_ref[pl.ds(n_near, n_first)] = kf_ref[...]
    vb_ref[pl.ds(n_near, n_first)] = vf_ref[0]
    for b in range(q_blocks):
        for j in range(slots):
            rows = pl.ds(j * BLK, BLK)
            kc_ref[rows, :] = kb_ref[sel_ref[b, j]]
            vc_ref[rows, :] = vb_ref[sel_ref[b, j]]
        qh = q_ref[pl.ds(b * BLK, BLK), :]
        s = lax.dot_general(
            kc_ref[...], qh, (((1,), (1,)), ((), ())), preferred_element_type=jnp.float32
        ) * scale
        top = jnp.max(s, axis=0, keepdims=True)
        w = jnp.exp(s - top)
        total = jnp.sum(w, axis=0, keepdims=True)
        acc = lax.dot_general(
            w.astype(jnp.bfloat16), vc_ref[...], (((0,), (0,)), ((), ())),
            preferred_element_type=jnp.float32,
        )
        total = jnp.transpose(jnp.broadcast_to(total, (BLK, BLK)))
        o_ref[pl.ds(b * BLK, BLK), :] = (acc / total).astype(o_ref.dtype)


def sparse_attend(sel, qn, kn_near, v_near, kn_first, first):
    tok_rows, width = qn.shape
    heads = width // HD
    q_blocks = tok_rows // BLK
    slots = sel.shape[1]
    n_near = kn_near.shape[0]
    n_first = kn_first.shape[0]
    kernel = functools.partial(attn_kernel, q_blocks=q_blocks, slots=slots)
    grid_spec = pltpu.PrefetchScalarGridSpec(
        num_scalar_prefetch=1,
        grid=(heads,),
        in_specs=[
            pl.BlockSpec((tok_rows, HD), lambda h, sel_ref: (0, h)),
            pl.BlockSpec(memory_space=pltpu.VMEM),
            pl.BlockSpec(memory_space=pltpu.VMEM),
            pl.BlockSpec((n_first, BLK, HD), lambda h, sel_ref: (0, 0, h)),
            pl.BlockSpec((1, n_first, BLK, HD), lambda h, sel_ref: (1, 0, 0, h)),
        ],
        out_specs=pl.BlockSpec((tok_rows, HD), lambda h, sel_ref: (0, h)),
        scratch_shapes=[
            pltpu.VMEM((slots * BLK, HD), jnp.bfloat16),
            pltpu.VMEM((slots * BLK, HD), jnp.bfloat16),
            pltpu.VMEM((n_near + n_first, BLK, HD), jnp.bfloat16),
            pltpu.VMEM((n_near + n_first, BLK, HD), jnp.bfloat16),
        ],
    )
    flops = 4 * q_blocks * slots * heads * BLK * BLK * HD
    return pl.pallas_call(
        kernel,
        grid_spec=grid_spec,
        out_shape=jax.ShapeDtypeStruct((tok_rows, width), jnp.bfloat16),
        compiler_params=pltpu.CompilerParams(vmem_limit_bytes=48 * 1024 * 1024),
        cost_estimate=pl.CostEstimate(
            flops=flops,
            transcendentals=q_blocks * slots * heads * BLK * BLK,
            bytes_accessed=2 * (2 * tok_rows * width + 2 * (n_near + n_first) * BLK * width),
        ),
    )(sel, qn, kn_near, v_near, kn_first, first)


def xor_gather(piece, n_frame, frame_pos):
    held = piece[None]
    bit = 1
    while bit < n_frame:
        perm = [(i, i ^ bit) for i in range(n_frame)]
        got = lax.ppermute(held, "frame", perm)
        upper = (frame_pos // bit) % 2 == 1
        held = jnp.where(
            upper, jnp.concatenate([got, held], axis=0), jnp.concatenate([held, got], axis=0)
        )
        bit *= 2
    return held


def xor_sum(x, axis, n):
    bit = 1
    while bit < n:
        perm = [(i, i ^ bit) for i in range(n)]
        x = x + lax.ppermute(x, axis, perm)
        bit *= 2
    return x


def body(q_proj, k_proj, v_proj, gain_q, gain_k, tiles, *, n_frame, n_tensor):
    tok_rows, width = q_proj.shape
    blocks = tok_rows // BLK
    frame_pos = lax.axis_index("frame")
    full_width = width * lax.axis_size("tensor")
    offsets = list(range(-NEAR, NEAR + 1))
    perms = {
        d: [(i, i - d) for i in range(n_frame) if 0 <= i - d < n_frame] for d in offsets if d != 0
    }

    kv_raw = jnp.stack([k_proj, v_proj])
    first = lax.all_gather(kv_raw[:, :BLK], "frame", axis=1, tiled=False)
    tail = kv_raw[:, BLK:]
    near = {0: tail}
    for d in perms:
        near[d] = lax.ppermute(tail, "frame", perms[d])

    q_wide = q_proj.astype(jnp.float32)
    k_wide = k_proj.astype(jnp.float32)
    row_sums = xor_sum(
        jnp.stack([jnp.sum(q_wide * q_wide, axis=1), jnp.sum(k_wide * k_wide, axis=1)]),
        "tensor",
        n_tensor,
    )
    q_norm = (q_wide * lax.rsqrt(row_sums[0] / full_width + EPS)[:, None] * gain_q).astype(
        jnp.bfloat16
    )
    k_sum = row_sums[1]
    all_sum = xor_gather(k_sum, n_frame, frame_pos)
    near_slab = jnp.clip(frame_pos + jnp.array(offsets), 0, n_frame - 1)
    near_sum = all_sum[near_slab][:, BLK:].reshape(len(offsets) * (blocks - 1), BLK)
    near_scale = lax.rsqrt(near_sum / full_width + EPS)[:, :, None]
    first_scale = lax.rsqrt(all_sum[:, :BLK] / full_width + EPS)[:, :, None]
    k_near = jnp.concatenate(
        [near[d][0].reshape(blocks - 1, BLK, width) for d in offsets], axis=0
    )
    kn_near = (k_near.astype(jnp.float32) * near_scale * gain_k).astype(jnp.bfloat16)
    v_near = jnp.concatenate(
        [near[d][1].reshape(blocks - 1, BLK, width) for d in offsets], axis=0
    )
    kn_first = (first[0].astype(jnp.float32) * first_scale * gain_k).astype(jnp.bfloat16)

    q_tiles = lax.dynamic_slice_in_dim(tiles, frame_pos * blocks, blocks, 0)
    key_slab = q_tiles // blocks
    within = q_tiles % blocks
    dist = key_slab - frame_pos
    near_ok = (jnp.abs(dist) <= NEAR) & (within > 0)
    near_idx = jnp.clip((dist + NEAR) * (blocks - 1) + within - 1, 0, len(offsets) * (blocks - 1) - 1)
    first_idx = jnp.clip(key_slab, 0, n_frame - 1)
    sel = jnp.where(near_ok, near_idx, len(offsets) * (blocks - 1) + first_idx).astype(jnp.int32)
    return sparse_attend(sel, q_norm, kn_near, v_near, kn_first, first)


def solution(mesh):
    return jax.shard_map(
        functools.partial(body, n_frame=mesh.shape["frame"], n_tensor=mesh.shape["tensor"]),
        mesh=mesh,
        in_specs=(
            P(("dp", "frame"), "tensor"),
            P(("dp", "frame"), "tensor"),
            P(("dp", "frame"), "tensor"),
            P("tensor"),
            P("tensor"),
            P("dp", None),
        ),
        out_specs=P(("dp", "frame"), "tensor"),
        check_vma=False,
    )
```
